1024 devices in a mesh: half: 2 (over x_hi), gx: 16 (over z), gy: 32 (over y, x_lo, core).
Axes of the slice: x: 4 (x_hi: 2, x_lo: 2; x = x_hi * 2 + x_lo), y: 8, z: 16, core: 2. Of those that a mesh axis runs over, the one named last changes fastest.
Arguments:
- state: float32 [2, 20, 32, 512, 128], P('half', None, 'gx', 'gy'), may hold values from -4 to 4
- levels: int32 [4, 32, 512], P(None, 'gx', 'gy'), may hold values from 0 to 128
- old_flux: float32 [2, 32, 512, 128], P(None, 'gx', 'gy'), may hold values from -4 to 4
- eco_prey: int32 [19], replicated, may hold values from 0 to 18
- eco_rate: float32 [19], replicated, may hold values from 0.3 to 3
Outputs:
- state_next: float32 [2, 20, 32, 512, 128], P('half', None, 'gx', 'gy')
The draws below stay inside these ranges and needn't reach their ends.
All inputs are finite; a program needn't handle non-finite values.
Results may differ from the reference program's by a relative error of at most 0.00013.
Values sent between devices are 32-bit elements; how exact they have to be, the bound alone decides.
No kernel may reach another device: no remote copies, remote signals or barrier semaphores. Data moves between devices by JAX's collectives and lax.ppermute only.
A program may use at most 32 MiB of HBM per device.

```python
import math
import jax
import jax.numpy as jnp
from jax import lax

K = 128
NT = 19
NSUB = 4
CHANNELS = 20
NXC = 32
NYC = 512


def with_ends(result, stream_key, low, high):
    longest = result.shape.index(max(result.shape))
    spots = []
    for shift in (0, 1):
        where = [jax.random.randint(jax.random.fold_in(stream_key, axis), (), 0, length) for axis, length in enumerate(result.shape)]
        where[longest] = (where[longest] + shift) % result.shape[longest]
        spots.append(tuple(where))
    return result.at[spots[0]].set(low).at[spots[1]].set(high)


def shard_levels(own_key, shape, cuts, smallest, top_value):
    level = 1.0
    for dim, shards_of in cuts:
        draws = jax.random.uniform(jax.random.fold_in(jax.random.fold_in(own_key, 6), dim), (shards_of,), jnp.float32, smallest / len(cuts), top_value / len(cuts))
        level = level * jnp.repeat(jnp.exp(draws), shape[dim] // shards_of).reshape((-1,) + (1,) * (len(shape) - 1 - dim))
    return level


def noise(rng, dims, width, reach, cuts=(), kind=jnp.bfloat16):
    values = width * jax.random.normal(rng, dims, jnp.float32)
    if cuts:
        values = values * shard_levels(rng, dims, cuts, -0.22, 0.18)
    return jnp.clip(values, -reach, reach).astype(kind)


def setup_inputs(seed: int = 0) -> dict:
    key_list = jax.random.split(jax.random.key(seed), 6)
    state = noise(key_list[0], (2, CHANNELS, NXC, NYC, K), 1.0, 4.0, ((0, 2), (2, 16), (3, 32)), jnp.float32)
    levels = with_ends(jax.random.randint(key_list[1], (4, NXC, NYC), 0, K + 1), jax.random.fold_in(key_list[1], 1), 0, K).astype(jnp.int32)
    old_flux = noise(key_list[2], (2, NXC, NYC, K), 1.0, 4.0, ((1, 16), (2, 32)), jnp.float32)
    eco_prey = with_ends(jax.random.randint(key_list[3], (NT,), 0, NT), jax.random.fold_in(key_list[3], 1), 0, NT - 1).astype(jnp.int32)
    eco_rate = jnp.clip(jnp.exp(jax.random.uniform(key_list[4], (NT,), jnp.float32, math.log(0.3), math.log(3.0))), 0.3, 3.0)
    return {"state": state, "levels": levels, "old_flux": old_flux, "eco_prey": eco_prey, "eco_rate": eco_rate}


DT = 0.1
NU = 1.0
CORIOLIS = 0.5
DRAG = 0.1
MORTALITY = 0.1
HEATING = 2.0
SURFACE = 8.0


def to_fine(coarse):
    fields = coarse.shape[0] // 4
    size_x, size_y, depth = coarse.shape[1], coarse.shape[2], coarse.shape[3]
    split = coarse.reshape(fields, 2, 2, size_x, size_y, depth).transpose(0, 3, 1, 4, 2, 5)
    return split.reshape(fields, 2 * size_x, 2 * size_y, depth)


def to_coarse(fine_cells):
    fields, fine_x, fine_y, depth = fine_cells.shape
    split = fine_cells.reshape(fields, fine_x // 2, 2, fine_y // 2, 2, depth).transpose(0, 2, 4, 1, 3, 5)
    return split.reshape(fields * 4, fine_x // 2, fine_y // 2, depth)


def fine_levels(levels):
    size_x, size_y = levels.shape[1], levels.shape[2]
    return levels.reshape(2, 2, size_x, size_y).transpose(2, 0, 3, 1).reshape(2 * size_x, 2 * size_y)


def wet_of(levels, depth):
    shape = levels.shape + (depth,)
    return (lax.broadcasted_iota(jnp.int32, shape, len(shape) - 1) < levels[..., None]).astype(jnp.float32)


def padded(fields):
    return jnp.pad(fields, ((0, 0), (1, 1), (1, 1), (0, 0)))


def ocean_substep(fields, wet_mask, heating):
    centre = fields[:, 1:-1, 1:-1]
    to_east = fields[:, 2:, 1:-1]
    to_west = fields[:, :-2, 1:-1]
    to_north = fields[:, 1:-1, 2:]
    to_south = fields[:, 1:-1, :-2]
    speed_east = centre[0]
    speed_north = centre[1]
    advect = speed_east * (to_east - to_west) * 0.5 + speed_north * (to_north - to_south) * 0.5
    spread = to_east + to_west + to_north + to_south - 4.0 * centre
    zeroes = jnp.zeros_like(speed_east)
    forcing = jnp.stack([CORIOLIS * speed_north - DRAG * speed_east, -CORIOLIS * speed_east - DRAG * speed_north, zeroes + heating, zeroes, zeroes + 1.0])
    return wet_mask * (centre + DT * (NU * spread - advect + forcing))


def tracer_substep(fields, wet_mask, volume_flux, eco_prey, eco_rate):
    species = eco_rate.shape[0]
    centre = fields[:, 1:-1, 1:-1]
    to_east = fields[:, 2:, 1:-1]
    to_west = fields[:, :-2, 1:-1]
    to_north = fields[:, 1:-1, 2:]
    to_south = fields[:, 1:-1, :-2]
    advect = volume_flux[0] * (to_east - to_west) * 0.5 + volume_flux[1] * (to_north - to_south) * 0.5
    spread = to_east + to_west + to_north + to_south - 4.0 * centre
    living = centre[:species]
    prey_values = living[eco_prey.astype(jnp.int32)]
    growth = eco_rate[:, None, None, None] * living * jnp.tanh(prey_values) - MORTALITY * living
    reaction = jnp.concatenate([growth, jnp.zeros_like(centre[species:])], axis=0)
    return wet_mask * (centre + DT * (NU * spread - advect + reaction))


def absorption(tracer, wet_mask):
    depth = tracer.shape[-1]
    above_table = (lax.broadcasted_iota(jnp.int32, (depth, depth), 0) < lax.broadcasted_iota(jnp.int32, (depth, depth), 1)).astype(jnp.float32)
    attenuation = wet_mask * (0.03 + 0.05 * jax.nn.softplus(tracer[0]))
    overhead = jnp.einsum("xyk,kl->xyl", attenuation, above_table, precision=lax.Precision.HIGHEST)
    return SURFACE * jnp.exp(-overhead) * (1.0 - jnp.exp(-attenuation))


def coarse_mean(fine_cells):
    fields, fine_x, fine_y, depth = fine_cells.shape
    return fine_cells.reshape(fields, fine_x // 2, 2, fine_y // 2, 2, depth).sum(axis=(2, 4)) * 0.25


def reference(state, levels, old_flux, eco_prey, eco_rate):
    depth = state.shape[-1]
    wet_fine = wet_of(fine_levels(levels), depth)
    wet_coarse = wet_of(jnp.max(levels, axis=0), depth)
    ocean_cells = to_fine(state[0]) * wet_fine
    tracer = state[1] * wet_coarse
    running = jnp.zeros((2,) + wet_coarse.shape, jnp.float32)
    for substep in range(NSUB):
        ocean_cells = ocean_substep(padded(ocean_cells), wet_fine, 0.0)
        running = running + coarse_mean(ocean_cells[0:2])
    for substep in range(NSUB):
        tracer = tracer_substep(padded(tracer), wet_coarse, old_flux, eco_prey, eco_rate)
    new_flux = running / NSUB
    absorbed = absorption(tracer, wet_coarse)
    heating = HEATING * jnp.repeat(jnp.repeat(absorbed, 2, axis=0), 2, axis=1)
    ocean_cells = ocean_substep(padded(ocean_cells), wet_fine, heating)
    tracer = tracer_substep(padded(tracer), wet_coarse, new_flux, eco_prey, eco_rate)
    return jnp.stack([to_coarse(ocean_cells), tracer])
```

```python
import jax
import jax.numpy as jnp
from jax import lax
from jax.sharding import PartitionSpec as P

NSUB = 4


DT = 0.1
NU = 1.0
CORIOLIS = 0.5
DRAG = 0.1
MORTALITY = 0.1
HEATING = 2.0
SURFACE = 8.0


def extended_2(shard, sides, width):
    pieces = []
    for axis, dim in sides:
        peers, length = (lax.axis_size(axis), shard.shape[dim])
        up = [(i, (i + 1) % peers) for i in range(peers - 1)]
        down = [(j, i) for i, j in up]
        last = lax.slice_in_dim(shard, length - width, length, axis=dim)
        leading = lax.slice_in_dim(shard, 0, width, axis=dim)
        pieces.append((dim, lax.ppermute(last, axis, up), lax.ppermute(leading, axis, down)))
    (dx, xb, xa), (dy, yb, ya) = pieces
    out = jnp.concatenate([xb, shard, xa], axis=dx)
    pad = [(0, 0)] * shard.ndim
    pad[dx] = (width, width)
    yb = jnp.pad(yb, pad)
    ya = jnp.pad(ya, pad)
    return jnp.concatenate([yb, out, ya], axis=dy)


def from_behind(shard, axis, by):
    peers = lax.axis_size(axis)
    pairs = [(i, i + by) for i in range(peers) if 0 <= i + by < peers]
    return lax.ppermute(shard, axis, pairs)


def to_fine(coarse):
    fields = coarse.shape[0] // 4
    size_x, size_y, depth = (coarse.shape[1], coarse.shape[2], coarse.shape[3])
    split = coarse.reshape(fields, 2, 2, size_x, size_y, depth).transpose(0, 3, 1, 4, 2, 5)
    return split.reshape(fields, 2 * size_x, 2 * size_y, depth)


def to_coarse(fine_cells):
    fields, fine_x, fine_y, depth = fine_cells.shape
    split = fine_cells.reshape(fields, fine_x // 2, 2, fine_y // 2, 2, depth).transpose(
        0, 2, 4, 1, 3, 5
    )
    return split.reshape(fields * 4, fine_x // 2, fine_y // 2, depth)


def fine_levels(levels):
    size_x, size_y = (levels.shape[1], levels.shape[2])
    return (
        levels.reshape(2, 2, size_x, size_y).transpose(2, 0, 3, 1).reshape(2 * size_x, 2 * size_y)
    )


def wet_of(levels, depth):
    shape = levels.shape + (depth,)
    return (lax.broadcasted_iota(jnp.int32, shape, len(shape) - 1) < levels[..., None]).astype(
        jnp.float32
    )


def trim_margin(values, margin, keep):
    cut = margin - keep
    if cut == 0:
        return values
    return values[..., cut : values.shape[-3] - cut, cut : values.shape[-2] - cut, :]


def ocean_substep(fields, wet_mask, heating):
    centre = fields[:, 1:-1, 1:-1]
    to_east = fields[:, 2:, 1:-1]
    to_west = fields[:, :-2, 1:-1]
    to_north = fields[:, 1:-1, 2:]
    to_south = fields[:, 1:-1, :-2]
    speed_east = centre[0]
    speed_north = centre[1]
    advect = speed_east * (to_east - to_west) * 0.5 + speed_north * (to_north - to_south) * 0.5
    spread = to_east + to_west + to_north + to_south - 4.0 * centre
    zeroes = jnp.zeros_like(speed_east)
    forcing = jnp.stack(
        [
            CORIOLIS * speed_north - DRAG * speed_east,
            -CORIOLIS * speed_east - DRAG * speed_north,
            zeroes + heating,
            zeroes,
            zeroes + 1.0,
        ]
    )
    return wet_mask * (centre + DT * (NU * spread - advect + forcing))


def tracer_substep(fields, wet_mask, volume_flux, onehot, eco_rate):
    species = eco_rate.shape[0]
    centre = fields[:, 1:-1, 1:-1]
    to_east = fields[:, 2:, 1:-1]
    to_west = fields[:, :-2, 1:-1]
    to_north = fields[:, 1:-1, 2:]
    to_south = fields[:, 1:-1, :-2]
    advect = (
        volume_flux[0] * (to_east - to_west) * 0.5 + volume_flux[1] * (to_north - to_south) * 0.5
    )
    spread = to_east + to_west + to_north + to_south - 4.0 * centre
    living = centre[:species]
    prey_values = jnp.einsum("ts,sxyk->txyk", onehot, living, precision=lax.Precision.HIGHEST)
    growth = eco_rate[:, None, None, None] * living * jnp.tanh(prey_values) - MORTALITY * living
    reaction = jnp.concatenate([growth, jnp.zeros_like(centre[species:])], axis=0)
    return wet_mask * (centre + DT * (NU * spread - advect + reaction))


def coarse_mean(fine_cells):
    coarse = to_coarse(fine_cells)
    return (
        coarse.reshape(
            fine_cells.shape[0], 4, coarse.shape[1], coarse.shape[2], coarse.shape[3]
        ).sum(axis=1)
        * 0.25
    )


def absorption(tracer, wet_mask, above_table):
    attenuation = wet_mask * (0.03 + 0.05 * jax.nn.softplus(tracer[0]))
    overhead = jnp.einsum("xyk,kl->xyl", attenuation, above_table, precision=lax.Precision.HIGHEST)
    return SURFACE * jnp.exp(-overhead) * (1.0 - jnp.exp(-attenuation))


def advance(
    is_ocean,
    extended,
    wide,
    steps,
    wet_fine,
    fine_margin,
    wet_coarse,
    coarse_margin,
    volume_flux,
    flux_margin,
    heating,
    running,
    onehot,
    eco_rate,
):

    def ocean_part():
        fine_cells = trim_margin(to_fine(extended), 2 * wide, steps)
        summed = running
        remain = steps - 1
        fine_cells = ocean_substep(fine_cells, trim_margin(wet_fine, fine_margin, remain), heating)
        summed = summed + coarse_mean(trim_margin(fine_cells[0:2], remain, 0))
        return (to_coarse(fine_cells), summed)

    def tracer_part():
        tracer = trim_margin(extended, wide, steps)
        remain = steps - 1
        tracer = tracer_substep(
            tracer,
            trim_margin(wet_coarse, coarse_margin, remain),
            trim_margin(volume_flux, flux_margin, remain),
            onehot,
            eco_rate,
        )
        return (tracer, running)

    return lax.cond(is_ocean, ocean_part, tracer_part)


def rim_single(own_block):
    return extended_2(own_block, (("gx", 1), ("gy", 2)), 1)


def body(state, levels, old_flux, eco_prey, eco_rate):
    depth = state.shape[-1]
    size_x, size_y = (state.shape[2], state.shape[3])
    species = eco_rate.shape[0]
    is_ocean = lax.axis_index("half") == 0
    onehot = (eco_prey[:, None] == lax.broadcasted_iota(jnp.int32, (species, species), 1)).astype(
        jnp.float32
    )
    above_table = (
        lax.broadcasted_iota(jnp.int32, (depth, depth), 0)
        < lax.broadcasted_iota(jnp.int32, (depth, depth), 1)
    ).astype(jnp.float32)
    wet_channels = wet_of(levels, depth)
    wet_fine = wet_of(fine_levels(levels), depth)
    wet_coarse = wet_of(jnp.max(levels, axis=0), depth)
    own_block = state[0]
    channels = own_block.shape[0]
    own_block = lax.cond(
        is_ocean,
        lambda: (
            own_block.reshape(channels // 4, 4, size_x, size_y, depth) * wet_channels[None]
        ).reshape(channels, size_x, size_y, depth),
        lambda: own_block * wet_coarse,
    )
    running = jnp.zeros((2, size_x, size_y, depth), jnp.float32)
    for substep in range(NSUB):
        extended = rim_single(own_block)
        own_block, running = advance(
            is_ocean,
            extended,
            1,
            1,
            wet_fine,
            0,
            wet_coarse,
            0,
            old_flux,
            0,
            0.0,
            running,
            onehot,
            eco_rate,
        )
    new_flux = running / NSUB
    absorbed = lax.cond(
        is_ocean,
        lambda: jnp.zeros((size_x, size_y, depth), jnp.float32),
        lambda: absorption(own_block, wet_coarse, above_table),
    )
    outgoing = jnp.where(is_ocean, new_flux, jnp.broadcast_to(absorbed[None], new_flux.shape))
    arrived = lax.ppermute(outgoing, "half", [(0, 1), (1, 0)])
    flux_arrived = arrived
    light_arrived = arrived[0:1]
    heating = HEATING * to_fine(jnp.broadcast_to(light_arrived, (4, size_x, size_y, depth)))[0]
    extended = rim_single(own_block)
    own_block, running = advance(
        is_ocean,
        extended,
        1,
        1,
        wet_fine,
        0,
        wet_coarse,
        0,
        flux_arrived,
        0,
        heating,
        running,
        onehot,
        eco_rate,
    )
    return own_block[None]


def solution(mesh):
    placed = (
        P("half", None, "gx", "gy", None),
        P(None, "gx", "gy"),
        P(None, "gx", "gy", None),
        P(),
        P(),
    )
    return jax.shard_map(
        body,
        mesh=mesh,
        in_specs=placed,
        out_specs=P("half", None, "gx", "gy", None),
        check_vma=False,
    )
```

```python
import jax
import jax.numpy as jnp
from jax import lax
from jax.sharding import PartitionSpec as P

NSUB = 4


DT = 0.1
NU = 1.0
CORIOLIS = 0.5
DRAG = 0.1
MORTALITY = 0.1
HEATING = 2.0
SURFACE = 8.0


def shifts(axis):
    peers = lax.axis_size(axis)
    up = [(i, i + 1) for i in range(peers - 1)]
    down = [(j, i) for i, j in up]
    return up, down


def halo_wide(block):
    up, down = shifts("gx")
    before = lax.ppermute(block, "gx", up)
    after = lax.ppermute(block, "gx", down)
    wide = jnp.concatenate([before, block, after], axis=1)
    rows = block.shape[1]
    up, down = shifts("gy")
    below = lax.ppermute(wide[:, :, -rows:], "gy", up)
    above = lax.ppermute(wide[:, :, :rows], "gy", down)
    return jnp.concatenate([below, wide, above], axis=2)


def halo_one(block):
    up, down = shifts("gx")
    xb = lax.ppermute(block[:, -1:], "gx", up)
    xa = lax.ppermute(block[:, :1], "gx", down)
    up, down = shifts("gy")
    yb = lax.ppermute(block[:, :, -1:], "gy", up)
    ya = lax.ppermute(block[:, :, :1], "gy", down)
    wide = jnp.concatenate([xb, block, xa], axis=1)
    pad = ((0, 0), (1, 1), (0, 0), (0, 0))
    return jnp.concatenate([jnp.pad(yb, pad), wide, jnp.pad(ya, pad)], axis=2)


def to_fine(coarse):
    fields = coarse.shape[0] // 4
    size_x, size_y, depth = (coarse.shape[1], coarse.shape[2], coarse.shape[3])
    split = coarse.reshape(fields, 2, 2, size_x, size_y, depth).transpose(0, 3, 1, 4, 2, 5)
    return split.reshape(fields, 2 * size_x, 2 * size_y, depth)


def to_coarse(fine_cells):
    fields, fine_x, fine_y, depth = fine_cells.shape
    split = fine_cells.reshape(fields, fine_x // 2, 2, fine_y // 2, 2, depth).transpose(
        0, 2, 4, 1, 3, 5
    )
    return split.reshape(fields * 4, fine_x // 2, fine_y // 2, depth)


def fine_levels(levels):
    size_x, size_y = (levels.shape[1], levels.shape[2])
    return (
        levels.reshape(2, 2, size_x, size_y).transpose(2, 0, 3, 1).reshape(2 * size_x, 2 * size_y)
    )


def wet_of(levels, depth):
    shape = levels.shape + (depth,)
    return (lax.broadcasted_iota(jnp.int32, shape, len(shape) - 1) < levels[..., None]).astype(
        jnp.float32
    )


def wet_of_float(levels, depth):
    shape = levels.shape + (depth,)
    return (
        lax.broadcasted_iota(jnp.int32, shape, len(shape) - 1).astype(jnp.float32)
        < levels[..., None]
    ).astype(jnp.float32)


def trim(values, cut):
    if cut == 0:
        return values
    return values[..., cut : values.shape[-3] - cut, cut : values.shape[-2] - cut, :]


def ocean_substep(fields, wet_mask, heating):
    centre = fields[:, 1:-1, 1:-1]
    to_east = fields[:, 2:, 1:-1]
    to_west = fields[:, :-2, 1:-1]
    to_north = fields[:, 1:-1, 2:]
    to_south = fields[:, 1:-1, :-2]
    speed_east = centre[0]
    speed_north = centre[1]
    advect = speed_east * (to_east - to_west) * 0.5 + speed_north * (to_north - to_south) * 0.5
    spread = to_east + to_west + to_north + to_south - 4.0 * centre
    zeroes = jnp.zeros_like(speed_east)
    forcing = jnp.stack(
        [
            CORIOLIS * speed_north - DRAG * speed_east,
            -CORIOLIS * speed_east - DRAG * speed_north,
            zeroes + heating,
            zeroes,
            zeroes + 1.0,
        ]
    )
    return wet_mask * (centre + DT * (NU * spread - advect + forcing))


def tracer_substep(fields, wet_mask, volume_flux, onehot, eco_rate):
    species = eco_rate.shape[0]
    centre = fields[:, 1:-1, 1:-1]
    to_east = fields[:, 2:, 1:-1]
    to_west = fields[:, :-2, 1:-1]
    to_north = fields[:, 1:-1, 2:]
    to_south = fields[:, 1:-1, :-2]
    advect = (
        volume_flux[0] * (to_east - to_west) * 0.5 + volume_flux[1] * (to_north - to_south) * 0.5
    )
    spread = to_east + to_west + to_north + to_south - 4.0 * centre
    living = centre[:species]
    prey_values = jnp.einsum("ts,sxyk->txyk", onehot, living, precision=lax.Precision.HIGHEST)
    growth = eco_rate[:, None, None, None] * living * jnp.tanh(prey_values) - MORTALITY * living
    reaction = jnp.concatenate([growth, jnp.zeros_like(centre[species:])], axis=0)
    return wet_mask * (centre + DT * (NU * spread - advect + reaction))


def coarse_mean(fine_cells):
    coarse = to_coarse(fine_cells)
    return (
        coarse.reshape(
            fine_cells.shape[0], 4, coarse.shape[1], coarse.shape[2], coarse.shape[3]
        ).sum(axis=1)
        * 0.25
    )


def absorption(tracer, wet_mask, above_table):
    attenuation = wet_mask * (0.03 + 0.05 * jax.nn.softplus(tracer[0]))
    overhead = jnp.einsum("xyk,kl->xyl", attenuation, above_table, precision=lax.Precision.HIGHEST)
    return SURFACE * jnp.exp(-overhead) * (1.0 - jnp.exp(-attenuation))


def body(state, levels, old_flux, eco_prey, eco_rate):
    depth = state.shape[-1]
    size_x, size_y = (state.shape[2], state.shape[3])
    species = eco_rate.shape[0]
    channels = state.shape[1]
    is_ocean = lax.axis_index("half") == 0
    onehot = (eco_prey[:, None] == lax.broadcasted_iota(jnp.int32, (species, species), 1)).astype(
        jnp.float32
    )
    above_table = (
        lax.broadcasted_iota(jnp.int32, (depth, depth), 0)
        < lax.broadcasted_iota(jnp.int32, (depth, depth), 1)
    ).astype(jnp.float32)
    wet_channels = wet_of(levels, depth)
    wet_fine = wet_of(fine_levels(levels), depth)
    wet_coarse = wet_of(jnp.max(levels, axis=0), depth)
    own_block = state[0]
    own_block = lax.cond(
        is_ocean,
        lambda: (
            own_block.reshape(channels // 4, 4, size_x, size_y, depth) * wet_channels[None]
        ).reshape(channels, size_x, size_y, depth),
        lambda: own_block * wet_coarse,
    )
    level_lanes = jnp.pad(
        levels.astype(jnp.float32).transpose(1, 2, 0), ((0, 0), (0, 0), (0, depth - 4))
    )[None]
    packed = jnp.concatenate([own_block, old_flux, level_lanes], axis=0)
    ext1 = halo_wide(packed)
    margin = (ext1.shape[1] - size_x) // 2
    state_ext = ext1[:channels]
    flux_ext = ext1[channels : channels + 2]
    levels_ext = ext1[channels + 2, :, :, 0:4].transpose(2, 0, 1)
    wet_coarse_ext = wet_of_float(jnp.max(levels_ext, axis=0), depth)
    wet_fine_ext = wet_of_float(fine_levels(levels_ext), depth)

    def ocean_a():
        fine = to_fine(state_ext)
        reach = 2 * margin
        running = jnp.zeros((2, size_x, size_y, depth), jnp.float32)
        for substep in range(NSUB):
            fine = ocean_substep(fine, trim(wet_fine_ext, substep + 1), 0.0)
            left = reach - substep - 1
            running = running + coarse_mean(trim(fine[0:2], left))
        return to_coarse(fine), running

    def tracer_a():
        tracer = state_ext
        for substep in range(margin):
            tracer = tracer_substep(
                tracer,
                trim(wet_coarse_ext, substep + 1),
                trim(flux_ext, substep + 1),
                onehot,
                eco_rate,
            )
        return tracer, jnp.zeros((2, size_x, size_y, depth), jnp.float32)

    block_a, running = lax.cond(is_ocean, ocean_a, tracer_a)
    ext2 = halo_wide(block_a)

    def ocean_b():
        return block_a, running / NSUB

    def tracer_b():
        tracer = ext2
        for substep in range(margin):
            tracer = tracer_substep(
                tracer,
                trim(wet_coarse_ext, substep + 1),
                trim(flux_ext, substep + 1),
                onehot,
                eco_rate,
            )
        absorbed = absorption(tracer, wet_coarse, above_table)
        return tracer, jnp.broadcast_to(absorbed[None], (2, size_x, size_y, depth))

    block_b, outgoing = lax.cond(is_ocean, ocean_b, tracer_b)
    ext3 = halo_one(block_b)
    arrived = lax.ppermute(outgoing, "half", [(0, 1), (1, 0)])

    def ocean_c():
        fine = trim(to_fine(ext3), 1)
        light = arrived[0:1]
        heating = HEATING * to_fine(jnp.broadcast_to(light, (4, size_x, size_y, depth)))[0]
        return to_coarse(ocean_substep(fine, wet_fine, heating))

    def tracer_c():
        return tracer_substep(ext3, wet_coarse, arrived, onehot, eco_rate)

    return lax.cond(is_ocean, ocean_c, tracer_c)[None]


def solution(mesh):
    placed = (
        P("half", None, "gx", "gy", None),
        P(None, "gx", "gy"),
        P(None, "gx", "gy", None),
        P(),
        P(),
    )
    return jax.shard_map(
        body,
        mesh=mesh,
        in_specs=placed,
        out_specs=P("half", None, "gx", "gy", None),
        check_vma=False,
    )
```

```python
import jax
import jax.numpy as jnp
from jax import lax
from jax.sharding import PartitionSpec as P

NSUB = 4


DT = 0.1
NU = 1.0
CORIOLIS = 0.5
DRAG = 0.1
MORTALITY = 0.1
HEATING = 2.0
SURFACE = 8.0


def shifts(axis):
    peers = lax.axis_size(axis)
    up = [(i, i + 1) for i in range(peers - 1)]
    down = [(j, i) for i, j in up]
    return up, down


def halo_wide(block):
    up, down = shifts("gx")
    before = lax.ppermute(block, "gx", up)
    after = lax.ppermute(block, "gx", down)
    wide = jnp.concatenate([before, block, after], axis=1)
    rows = block.shape[1]
    up, down = shifts("gy")
    below = lax.ppermute(wide[:, :, -rows:], "gy", up)
    above = lax.ppermute(wide[:, :, :rows], "gy", down)
    return jnp.concatenate([below, wide, above], axis=2)


def halo_three(block):
    up, down = shifts("gx")
    peers = lax.axis_size("gx")
    up2 = [(i, i + 2) for i in range(peers - 2)]
    down2 = [(j, i) for i, j in up2]
    b1 = lax.ppermute(block, "gx", up)
    a1 = lax.ppermute(block, "gx", down)
    b2 = lax.ppermute(block[:, -1:], "gx", up2)
    a2 = lax.ppermute(block[:, :1], "gx", down2)
    wide = jnp.concatenate([b2, b1, block, a1, a2], axis=1)
    up, down = shifts("gy")
    below = lax.ppermute(wide[:, :, -3:], "gy", up)
    above = lax.ppermute(wide[:, :, :3], "gy", down)
    return jnp.concatenate([below, wide, above], axis=2)


def halo_one(block):
    up, down = shifts("gx")
    xb = lax.ppermute(block[:, -1:], "gx", up)
    xa = lax.ppermute(block[:, :1], "gx", down)
    up, down = shifts("gy")
    yb = lax.ppermute(block[:, :, -1:], "gy", up)
    ya = lax.ppermute(block[:, :, :1], "gy", down)
    wide = jnp.concatenate([xb, block, xa], axis=1)
    pad = ((0, 0), (1, 1), (0, 0), (0, 0))
    return jnp.concatenate([jnp.pad(yb, pad), wide, jnp.pad(ya, pad)], axis=2)


def to_fine(coarse):
    fields = coarse.shape[0] // 4
    size_x, size_y, depth = (coarse.shape[1], coarse.shape[2], coarse.shape[3])
    split = coarse.reshape(fields, 2, 2, size_x, size_y, depth).transpose(0, 3, 1, 4, 2, 5)
    return split.reshape(fields, 2 * size_x, 2 * size_y, depth)


def to_coarse(fine_cells):
    fields, fine_x, fine_y, depth = fine_cells.shape
    split = fine_cells.reshape(fields, fine_x // 2, 2, fine_y // 2, 2, depth).transpose(
        0, 2, 4, 1, 3, 5
    )
    return split.reshape(fields * 4, fine_x // 2, fine_y // 2, depth)


def fine_levels(levels):
    size_x, size_y = (levels.shape[1], levels.shape[2])
    return (
        levels.reshape(2, 2, size_x, size_y).transpose(2, 0, 3, 1).reshape(2 * size_x, 2 * size_y)
    )


def wet_of(levels, depth):
    shape = levels.shape + (depth,)
    return (lax.broadcasted_iota(jnp.int32, shape, len(shape) - 1) < levels[..., None]).astype(
        jnp.float32
    )


def wet_of_float(levels, depth):
    shape = levels.shape + (depth,)
    return (
        lax.broadcasted_iota(jnp.int32, shape, len(shape) - 1).astype(jnp.float32)
        < levels[..., None]
    ).astype(jnp.float32)


def trim(values, cut):
    if cut == 0:
        return values
    return values[..., cut : values.shape[-3] - cut, cut : values.shape[-2] - cut, :]


def ocean_substep(fields, wet_mask, heating):
    centre = fields[:, 1:-1, 1:-1]
    to_east = fields[:, 2:, 1:-1]
    to_west = fields[:, :-2, 1:-1]
    to_north = fields[:, 1:-1, 2:]
    to_south = fields[:, 1:-1, :-2]
    speed_east = centre[0]
    speed_north = centre[1]
    advect = speed_east * (to_east - to_west) * 0.5 + speed_north * (to_north - to_south) * 0.5
    spread = to_east + to_west + to_north + to_south - 4.0 * centre
    zeroes = jnp.zeros_like(speed_east)
    forcing = jnp.stack(
        [
            CORIOLIS * speed_north - DRAG * speed_east,
            -CORIOLIS * speed_east - DRAG * speed_north,
            zeroes + heating,
            zeroes,
            zeroes + 1.0,
        ]
    )
    return wet_mask * (centre + DT * (NU * spread - advect + forcing))


def tracer_substep(fields, wet_mask, volume_flux, onehot, eco_rate):
    species = eco_rate.shape[0]
    centre = fields[:, 1:-1, 1:-1]
    to_east = fields[:, 2:, 1:-1]
    to_west = fields[:, :-2, 1:-1]
    to_north = fields[:, 1:-1, 2:]
    to_south = fields[:, 1:-1, :-2]
    advect = (
        volume_flux[0] * (to_east - to_west) * 0.5 + volume_flux[1] * (to_north - to_south) * 0.5
    )
    spread = to_east + to_west + to_north + to_south - 4.0 * centre
    living = centre[:species]
    prey_values = jnp.einsum("ts,sxyk->txyk", onehot, living, precision=lax.Precision.HIGHEST)
    growth = eco_rate[:, None, None, None] * living * jnp.tanh(prey_values) - MORTALITY * living
    reaction = jnp.concatenate([growth, jnp.zeros_like(centre[species:])], axis=0)
    return wet_mask * (centre + DT * (NU * spread - advect + reaction))


def coarse_mean(fine_cells):
    coarse = to_coarse(fine_cells)
    return (
        coarse.reshape(
            fine_cells.shape[0], 4, coarse.shape[1], coarse.shape[2], coarse.shape[3]
        ).sum(axis=1)
        * 0.25
    )


def absorption(tracer, wet_mask, above_table):
    attenuation = wet_mask * (0.03 + 0.05 * jax.nn.softplus(tracer[0]))
    overhead = jnp.einsum("xyk,kl->xyl", attenuation, above_table, precision=lax.Precision.HIGHEST)
    return SURFACE * jnp.exp(-overhead) * (1.0 - jnp.exp(-attenuation))


def body(state, levels, old_flux, eco_prey, eco_rate):
    depth = state.shape[-1]
    size_x, size_y = (state.shape[2], state.shape[3])
    species = eco_rate.shape[0]
    channels = state.shape[1]
    is_ocean = lax.axis_index("half") == 0
    level_lanes = jnp.pad(
        levels.astype(jnp.float32).transpose(1, 2, 0), ((0, 0), (0, 0), (0, depth - 4))
    )[None]
    packed = jnp.concatenate([state[0], old_flux, level_lanes], axis=0)
    ext1 = halo_wide(packed)
    margin = (ext1.shape[1] - size_x) // 2
    onehot = (eco_prey[:, None] == lax.broadcasted_iota(jnp.int32, (species, species), 1)).astype(
        jnp.float32
    )
    above_table = (
        lax.broadcasted_iota(jnp.int32, (depth, depth), 0)
        < lax.broadcasted_iota(jnp.int32, (depth, depth), 1)
    ).astype(jnp.float32)
    wet_fine = wet_of(fine_levels(levels), depth)
    wet_coarse = wet_of(jnp.max(levels, axis=0), depth)
    raw_ext = ext1[:channels]
    flux_ext = ext1[channels : channels + 2]
    levels_ext = ext1[channels + 2, :, :, 0:4].transpose(2, 0, 1)
    wet_coarse_ext = wet_of_float(jnp.max(levels_ext, axis=0), depth)
    wet_fine_ext = wet_of_float(fine_levels(levels_ext), depth)
    zeros_flux = jnp.zeros((2, size_x, size_y, depth), jnp.float32)

    def ocean_a():
        fine = to_fine(raw_ext) * wet_fine_ext[None]
        reach = 2 * margin
        running = zeros_flux
        for substep in range(2):
            fine = ocean_substep(fine, trim(wet_fine_ext, substep + 1), 0.0)
            running = running + coarse_mean(trim(fine[0:2], reach - substep - 1))
        return to_coarse(trim(fine, reach - 2)), running

    def tracer_a():
        tracer = raw_ext * wet_coarse_ext[None]
        for substep in range(margin):
            tracer = tracer_substep(
                tracer,
                trim(wet_coarse_ext, substep + 1),
                trim(flux_ext, substep + 1),
                onehot,
                eco_rate,
            )
        return tracer, zeros_flux

    block_a, running = lax.cond(is_ocean, ocean_a, tracer_a)
    ext2 = halo_three(block_a)
    reach2 = (ext2.shape[1] - size_x) // 2
    tracer_shape = (channels, size_x + 2, size_y + 2, depth)
    ocean_shape = (channels // 4, 2 * size_x + 2, 2 * size_y + 2, depth)

    def ocean_b():
        fine = trim(to_fine(ext2), 2 * reach2 - 3)
        summed = running
        for substep in range(2):
            fine = ocean_substep(fine, trim(wet_fine_ext, 2 * margin - 2 + substep), 0.0)
            summed = summed + coarse_mean(trim(fine[0:2], 2 - substep))
        return jnp.zeros(tracer_shape, jnp.float32), fine, summed / NSUB

    def tracer_b():
        tracer = ext2
        for substep in range(2):
            tracer = tracer_substep(
                tracer,
                trim(wet_coarse_ext, substep),
                trim(flux_ext, substep),
                onehot,
                eco_rate,
            )
        absorbed = absorption(trim(tracer, 1), wet_coarse, above_table)
        outgoing = jnp.broadcast_to(absorbed[None], (2, size_x, size_y, depth))
        return tracer, jnp.zeros(ocean_shape, jnp.float32), outgoing

    tracer_b4, ocean_b4, outgoing = lax.cond(is_ocean, ocean_b, tracer_b)
    arrived = lax.ppermute(outgoing, "half", [(0, 1), (1, 0)])

    def ocean_c():
        light = arrived[0:1]
        heating = HEATING * to_fine(jnp.broadcast_to(light, (4, size_x, size_y, depth)))[0]
        return to_coarse(ocean_substep(ocean_b4, wet_fine, heating))

    def tracer_c():
        return tracer_substep(tracer_b4, wet_coarse, arrived, onehot, eco_rate)

    return lax.cond(is_ocean, ocean_c, tracer_c)[None]


def solution(mesh):
    placed = (
        P("half", None, "gx", "gy", None),
        P(None, "gx", "gy"),
        P(None, "gx", "gy", None),
        P(),
        P(),
    )
    return jax.shard_map(
        body,
        mesh=mesh,
        in_specs=placed,
        out_specs=P("half", None, "gx", "gy", None),
        check_vma=False,
    )
```

```python
import jax
import jax.numpy as jnp
from jax import lax
from jax.sharding import PartitionSpec as P

NSUB = 4


DT = 0.1
NU = 1.0
CORIOLIS = 0.5
DRAG = 0.1
MORTALITY = 0.1
HEATING = 2.0
SURFACE = 8.0


def shifts(axis):
    peers = lax.axis_size(axis)
    up = [(i, i + 1) for i in range(peers - 1)]
    down = [(j, i) for i, j in up]
    return up, down


def halo_wide(block):
    up, down = shifts("gx")
    peers = lax.axis_size("gx")
    up2 = [(i, i + 2) for i in range(peers - 2)]
    down2 = [(j, i) for i, j in up2]
    b1 = lax.ppermute(block, "gx", up)
    a1 = lax.ppermute(block, "gx", down)
    b2 = lax.ppermute(block, "gx", up2)
    a2 = lax.ppermute(block, "gx", down2)
    wide = jnp.concatenate([b2, b1, block, a1, a2], axis=1)
    rows = 2 * block.shape[1]
    up, down = shifts("gy")
    below = lax.ppermute(wide[:, :, -rows:], "gy", up)
    above = lax.ppermute(wide[:, :, :rows], "gy", down)
    return jnp.concatenate([below, wide, above], axis=2)


def halo_one(block):
    up, down = shifts("gx")
    xb = lax.ppermute(block[:, -1:], "gx", up)
    xa = lax.ppermute(block[:, :1], "gx", down)
    up, down = shifts("gy")
    yb = lax.ppermute(block[:, :, -1:], "gy", up)
    ya = lax.ppermute(block[:, :, :1], "gy", down)
    wide = jnp.concatenate([xb, block, xa], axis=1)
    pad = ((0, 0), (1, 1), (0, 0), (0, 0))
    return jnp.concatenate([jnp.pad(yb, pad), wide, jnp.pad(ya, pad)], axis=2)


def to_fine(coarse):
    fields = coarse.shape[0] // 4
    size_x, size_y, depth = (coarse.shape[1], coarse.shape[2], coarse.shape[3])
    split = coarse.reshape(fields, 2, 2, size_x, size_y, depth).transpose(0, 3, 1, 4, 2, 5)
    return split.reshape(fields, 2 * size_x, 2 * size_y, depth)


def to_coarse(fine_cells):
    fields, fine_x, fine_y, depth = fine_cells.shape
    split = fine_cells.reshape(fields, fine_x // 2, 2, fine_y // 2, 2, depth).transpose(
        0, 2, 4, 1, 3, 5
    )
    return split.reshape(fields * 4, fine_x // 2, fine_y // 2, depth)


def fine_levels(levels):
    size_x, size_y = (levels.shape[1], levels.shape[2])
    return (
        levels.reshape(2, 2, size_x, size_y).transpose(2, 0, 3, 1).reshape(2 * size_x, 2 * size_y)
    )


def wet_of(levels, depth):
    shape = levels.shape + (depth,)
    return (lax.broadcasted_iota(jnp.int32, shape, len(shape) - 1) < levels[..., None]).astype(
        jnp.float32
    )


def wet_of_float(levels, depth):
    shape = levels.shape + (depth,)
    return (
        lax.broadcasted_iota(jnp.int32, shape, len(shape) - 1).astype(jnp.float32)
        < levels[..., None]
    ).astype(jnp.float32)


def trim(values, cut):
    if cut == 0:
        return values
    return values[..., cut : values.shape[-3] - cut, cut : values.shape[-2] - cut, :]


def ocean_substep(fields, wet_mask, heating):
    centre = fields[:, 1:-1, 1:-1]
    to_east = fields[:, 2:, 1:-1]
    to_west = fields[:, :-2, 1:-1]
    to_north = fields[:, 1:-1, 2:]
    to_south = fields[:, 1:-1, :-2]
    speed_east = centre[0]
    speed_north = centre[1]
    advect = speed_east * (to_east - to_west) * 0.5 + speed_north * (to_north - to_south) * 0.5
    spread = to_east + to_west + to_north + to_south - 4.0 * centre
    zeroes = jnp.zeros_like(speed_east)
    forcing = jnp.stack(
        [
            CORIOLIS * speed_north - DRAG * speed_east,
            -CORIOLIS * speed_east - DRAG * speed_north,
            zeroes + heating,
            zeroes,
            zeroes + 1.0,
        ]
    )
    return wet_mask * (centre + DT * (NU * spread - advect + forcing))


def tracer_substep(fields, wet_mask, volume_flux, onehot, eco_rate):
    species = eco_rate.shape[0]
    centre = fields[:, 1:-1, 1:-1]
    to_east = fields[:, 2:, 1:-1]
    to_west = fields[:, :-2, 1:-1]
    to_north = fields[:, 1:-1, 2:]
    to_south = fields[:, 1:-1, :-2]
    advect = (
        volume_flux[0] * (to_east - to_west) * 0.5 + volume_flux[1] * (to_north - to_south) * 0.5
    )
    spread = to_east + to_west + to_north + to_south - 4.0 * centre
    living = centre[:species]
    prey_values = jnp.einsum("ts,sxyk->txyk", onehot, living, precision=lax.Precision.HIGHEST)
    growth = eco_rate[:, None, None, None] * living * jnp.tanh(prey_values) - MORTALITY * living
    reaction = jnp.concatenate([growth, jnp.zeros_like(centre[species:])], axis=0)
    return wet_mask * (centre + DT * (NU * spread - advect + reaction))


def coarse_mean(fine_cells):
    coarse = to_coarse(fine_cells)
    return (
        coarse.reshape(
            fine_cells.shape[0], 4, coarse.shape[1], coarse.shape[2], coarse.shape[3]
        ).sum(axis=1)
        * 0.25
    )


def absorption(tracer, wet_mask, above_table):
    attenuation = wet_mask * (0.03 + 0.05 * jax.nn.softplus(tracer[0]))
    overhead = jnp.einsum("xyk,kl->xyl", attenuation, above_table, precision=lax.Precision.HIGHEST)
    return SURFACE * jnp.exp(-overhead) * (1.0 - jnp.exp(-attenuation))


def body(state, levels, old_flux, eco_prey, eco_rate):
    depth = state.shape[-1]
    size_x, size_y = (state.shape[2], state.shape[3])
    species = eco_rate.shape[0]
    channels = state.shape[1]
    is_ocean = lax.axis_index("half") == 0
    onehot = (eco_prey[:, None] == lax.broadcasted_iota(jnp.int32, (species, species), 1)).astype(
        jnp.float32
    )
    above_table = (
        lax.broadcasted_iota(jnp.int32, (depth, depth), 0)
        < lax.broadcasted_iota(jnp.int32, (depth, depth), 1)
    ).astype(jnp.float32)
    wet_channels = wet_of(levels, depth)
    wet_fine = wet_of(fine_levels(levels), depth)
    wet_coarse = wet_of(jnp.max(levels, axis=0), depth)
    own_block = state[0]
    own_block = lax.cond(
        is_ocean,
        lambda: (
            own_block.reshape(channels // 4, 4, size_x, size_y, depth) * wet_channels[None]
        ).reshape(channels, size_x, size_y, depth),
        lambda: own_block * wet_coarse,
    )
    level_lanes = jnp.pad(
        levels.astype(jnp.float32).transpose(1, 2, 0), ((0, 0), (0, 0), (0, depth - 4))
    )[None]
    packed = jnp.concatenate([own_block, old_flux, level_lanes], axis=0)
    ext1 = halo_wide(packed)
    margin = (ext1.shape[1] - size_x) // 2
    state_ext = ext1[:channels]
    flux_ext = ext1[channels : channels + 2]
    levels_ext = ext1[channels + 2, :, :, 0:4].transpose(2, 0, 1)
    wet_coarse_ext = wet_of_float(jnp.max(levels_ext, axis=0), depth)
    wet_fine_ext = wet_of_float(fine_levels(levels_ext), depth)

    def ocean_a():
        fine = trim(to_fine(state_ext), 2 * margin - NSUB - 1)
        running = jnp.zeros((2, size_x, size_y, depth), jnp.float32)
        for substep in range(NSUB):
            fine = ocean_substep(fine, trim(wet_fine_ext, 2 * margin - NSUB + substep), 0.0)
            running = running + coarse_mean(trim(fine[0:2], NSUB - substep))
        return jnp.zeros((channels, size_x, size_y, depth), jnp.float32), fine, running / NSUB

    def tracer_a():
        tracer = state_ext
        for substep in range(margin):
            tracer = tracer_substep(
                tracer,
                trim(wet_coarse_ext, substep + 1),
                trim(flux_ext, substep + 1),
                onehot,
                eco_rate,
            )
        absorbed = absorption(tracer, wet_coarse, above_table)
        outgoing = jnp.broadcast_to(absorbed[None], (2, size_x, size_y, depth))
        fine_shape = (channels // 4, 2 * size_x + 2, 2 * size_y + 2, depth)
        return tracer, jnp.zeros(fine_shape, jnp.float32), outgoing

    tracer_blk, ocean_fine, outgoing = lax.cond(is_ocean, ocean_a, tracer_a)
    ext3 = halo_one(tracer_blk)
    arrived = lax.ppermute(outgoing, "half", [(0, 1), (1, 0)])

    def ocean_c():
        light = arrived[0:1]
        heating = HEATING * to_fine(jnp.broadcast_to(light, (4, size_x, size_y, depth)))[0]
        return to_coarse(ocean_substep(ocean_fine, wet_fine, heating))

    def tracer_c():
        return tracer_substep(ext3, wet_coarse, arrived, onehot, eco_rate)

    return lax.cond(is_ocean, ocean_c, tracer_c)[None]


def solution(mesh):
    placed = (
        P("half", None, "gx", "gy", None),
        P(None, "gx", "gy"),
        P(None, "gx", "gy", None),
        P(),
        P(),
    )
    return jax.shard_map(
        body,
        mesh=mesh,
        in_specs=placed,
        out_specs=P("half", None, "gx", "gy", None),
        check_vma=False,
    )
```

```python
import jax
import jax.numpy as jnp
from jax import lax
from jax.sharding import PartitionSpec as P

NSUB = 4


DT = 0.1
NU = 1.0
CORIOLIS = 0.5
DRAG = 0.1
MORTALITY = 0.1
HEATING = 2.0
SURFACE = 8.0


def shifts(axis):
    peers = lax.axis_size(axis)
    up = [(i, i + 1) for i in range(peers - 1)]
    down = [(j, i) for i, j in up]
    return up, down


def halo_x(block, cells):
    up, down = shifts("gx")
    before = lax.ppermute(block[:, block.shape[1] - cells :], "gx", up)
    after = lax.ppermute(block[:, :cells], "gx", down)
    return jnp.concatenate([before, block, after], axis=1)


def halo_y(block, rows):
    up, down = shifts("gy")
    below = lax.ppermute(block[:, :, block.shape[2] - rows :], "gy", up)
    above = lax.ppermute(block[:, :, :rows], "gy", down)
    return jnp.concatenate([below, block, above], axis=2)


def to_fine(coarse):
    fields = coarse.shape[0] // 4
    size_x, size_y, depth = (coarse.shape[1], coarse.shape[2], coarse.shape[3])
    split = coarse.reshape(fields, 2, 2, size_x, size_y, depth).transpose(0, 3, 1, 4, 2, 5)
    return split.reshape(fields, 2 * size_x, 2 * size_y, depth)


def to_coarse(fine_cells):
    fields, fine_x, fine_y, depth = fine_cells.shape
    split = fine_cells.reshape(fields, fine_x // 2, 2, fine_y // 2, 2, depth).transpose(
        0, 2, 4, 1, 3, 5
    )
    return split.reshape(fields * 4, fine_x // 2, fine_y // 2, depth)


def fine_levels(levels):
    size_x, size_y = (levels.shape[1], levels.shape[2])
    return (
        levels.reshape(2, 2, size_x, size_y).transpose(2, 0, 3, 1).reshape(2 * size_x, 2 * size_y)
    )


def wet_of(levels, depth):
    shape = levels.shape + (depth,)
    return (lax.broadcasted_iota(jnp.int32, shape, len(shape) - 1) < levels[..., None]).astype(
        jnp.float32
    )


def wet_of_float(levels, depth):
    shape = levels.shape + (depth,)
    return (
        lax.broadcasted_iota(jnp.int32, shape, len(shape) - 1).astype(jnp.float32)
        < levels[..., None]
    ).astype(jnp.float32)


def trim(values, cut, cut_y=None):
    cut_y = cut if cut_y is None else cut_y
    return values[..., cut : values.shape[-3] - cut, cut_y : values.shape[-2] - cut_y, :]


def ocean_substep(fields, wet_mask, heating):
    centre = fields[:, 1:-1, 1:-1]
    to_east = fields[:, 2:, 1:-1]
    to_west = fields[:, :-2, 1:-1]
    to_north = fields[:, 1:-1, 2:]
    to_south = fields[:, 1:-1, :-2]
    speed_east = centre[0]
    speed_north = centre[1]
    advect = speed_east * (to_east - to_west) * 0.5 + speed_north * (to_north - to_south) * 0.5
    spread = to_east + to_west + to_north + to_south - 4.0 * centre
    zeroes = jnp.zeros_like(speed_east)
    forcing = jnp.stack(
        [
            CORIOLIS * speed_north - DRAG * speed_east,
            -CORIOLIS * speed_east - DRAG * speed_north,
            zeroes + heating,
            zeroes,
            zeroes + 1.0,
        ]
    )
    return wet_mask * (centre + DT * (NU * spread - advect + forcing))


def tracer_substep(fields, wet_mask, volume_flux, onehot, eco_rate):
    species = eco_rate.shape[0]
    centre = fields[:, 1:-1, 1:-1]
    to_east = fields[:, 2:, 1:-1]
    to_west = fields[:, :-2, 1:-1]
    to_north = fields[:, 1:-1, 2:]
    to_south = fields[:, 1:-1, :-2]
    advect = (
        volume_flux[0] * (to_east - to_west) * 0.5 + volume_flux[1] * (to_north - to_south) * 0.5
    )
    spread = to_east + to_west + to_north + to_south - 4.0 * centre
    living = centre[:species]
    prey_values = jnp.einsum("ts,sxyk->txyk", onehot, living, precision=lax.Precision.HIGHEST)
    growth = eco_rate[:, None, None, None] * living * jnp.tanh(prey_values) - MORTALITY * living
    reaction = jnp.concatenate([growth, jnp.zeros_like(centre[species:])], axis=0)
    return wet_mask * (centre + DT * (NU * spread - advect + reaction))


def coarse_mean(fine_cells):
    coarse = to_coarse(fine_cells)
    return (
        coarse.reshape(
            fine_cells.shape[0], 4, coarse.shape[1], coarse.shape[2], coarse.shape[3]
        ).sum(axis=1)
        * 0.25
    )


def absorption(tracer, wet_mask, above_table):
    attenuation = wet_mask * (0.03 + 0.05 * jax.nn.softplus(tracer[0]))
    overhead = jnp.einsum("xyk,kl->xyl", attenuation, above_table, precision=lax.Precision.HIGHEST)
    return SURFACE * jnp.exp(-overhead) * (1.0 - jnp.exp(-attenuation))


def body(state, levels, old_flux, eco_prey, eco_rate):
    depth = state.shape[-1]
    size_x, size_y = (state.shape[2], state.shape[3])
    species = eco_rate.shape[0]
    channels = state.shape[1]
    is_ocean = lax.axis_index("half") == 0
    level_lanes = jnp.pad(
        levels.astype(jnp.float32).transpose(1, 2, 0), ((0, 0), (0, 0), (0, depth - 4))
    )[None]
    packed = jnp.concatenate([state[0], old_flux, level_lanes], axis=0)
    reach_x, reach_y = size_x, NSUB + 1
    ext1 = halo_y(halo_x(packed, reach_x), reach_y)
    onehot = (eco_prey[:, None] == lax.broadcasted_iota(jnp.int32, (species, species), 1)).astype(
        jnp.float32
    )
    above_table = (
        lax.broadcasted_iota(jnp.int32, (depth, depth), 0)
        < lax.broadcasted_iota(jnp.int32, (depth, depth), 1)
    ).astype(jnp.float32)
    wet_fine = wet_of(fine_levels(levels), depth)
    wet_coarse = wet_of(jnp.max(levels, axis=0), depth)
    raw_ext = ext1[:channels]
    flux_ext = ext1[channels : channels + 2]
    levels_ext = ext1[channels + 2, :, :, 0:4].transpose(2, 0, 1)
    wet_coarse_ext = wet_of_float(jnp.max(levels_ext, axis=0), depth)
    wet_fine_ext = wet_of_float(fine_levels(levels_ext), depth)
    zeros_flux = jnp.zeros((2, size_x, size_y, depth), jnp.float32)
    mid_y, late_y = reach_y - 2, reach_y - 4
    shape_mid = (channels, size_x, size_y + 2 * mid_y, depth)
    shape_late = (channels, size_x, size_y + 2 * late_y, depth)

    def ocean_a():
        keep_y = NSUB + 2 * late_y
        fine = trim(to_fine(raw_ext) * wet_fine_ext[None], 0, 2 * reach_y - keep_y)
        running = zeros_flux
        for substep in range(NSUB):
            fine = ocean_substep(
                fine, trim(wet_fine_ext, substep + 1, 2 * reach_y - keep_y + substep + 1), 0.0
            )
            running = running + coarse_mean(
                trim(fine[0:2], 2 * reach_x - substep - 1, keep_y - substep - 1)
            )
        return jnp.zeros(shape_mid, jnp.float32), to_coarse(fine), running

    def tracer_a():
        tracer = raw_ext * wet_coarse_ext[None]
        for substep in range(2):
            tracer = tracer_substep(
                tracer,
                trim(wet_coarse_ext, substep + 1),
                trim(flux_ext, substep + 1),
                onehot,
                eco_rate,
            )
        return tracer, jnp.zeros(shape_late, jnp.float32), zeros_flux

    block_mid, ocean_late, running = lax.cond(is_ocean, ocean_a, tracer_a)
    ext2 = halo_x(block_mid, reach_x)

    def ocean_b():
        return ocean_late, running / NSUB

    def tracer_b():
        tracer = ext2
        for substep in range(2):
            tracer = tracer_substep(
                tracer,
                trim(wet_coarse_ext, substep + 1, reach_y - mid_y + substep + 1),
                trim(flux_ext, substep + 1, reach_y - mid_y + substep + 1),
                onehot,
                eco_rate,
            )
        absorbed = absorption(trim(tracer, 0, late_y), wet_coarse, above_table)
        return tracer, jnp.broadcast_to(absorbed[None], (2, size_x, size_y, depth))

    block_late, outgoing = lax.cond(is_ocean, ocean_b, tracer_b)
    ext3 = halo_x(block_late, 1)
    arrived = lax.ppermute(outgoing, "half", [(0, 1), (1, 0)])

    def ocean_c():
        fine = trim(to_fine(ext3), 1, 2 * late_y - 1)
        light = arrived[0:1]
        heating = HEATING * to_fine(jnp.broadcast_to(light, (4, size_x, size_y, depth)))[0]
        return to_coarse(ocean_substep(fine, wet_fine, heating))

    def tracer_c():
        return tracer_substep(trim(ext3, 0, late_y - 1), wet_coarse, arrived, onehot, eco_rate)

    return lax.cond(is_ocean, ocean_c, tracer_c)[None]


def solution(mesh):
    placed = (
        P("half", None, "gx", "gy", None),
        P(None, "gx", "gy"),
        P(None, "gx", "gy", None),
        P(),
        P(),
    )
    return jax.shard_map(
        body,
        mesh=mesh,
        in_specs=placed,
        out_specs=P("half", None, "gx", "gy", None),
        check_vma=False,
    )
```

```python
import jax
import jax.numpy as jnp
from jax import lax
from jax.sharding import PartitionSpec as P

NSUB = 4


DT = 0.1
NU = 1.0
CORIOLIS = 0.5
DRAG = 0.1
MORTALITY = 0.1
HEATING = 2.0
SURFACE = 8.0


def shifts(axis):
    peers = lax.axis_size(axis)
    up = [(i, i + 1) for i in range(peers - 1)]
    down = [(j, i) for i, j in up]
    return up, down


def halo_x(block, cells):
    up, down = shifts("gx")
    before = lax.ppermute(block[:, block.shape[1] - cells :], "gx", up)
    after = lax.ppermute(block[:, :cells], "gx", down)
    return jnp.concatenate([before, block, after], axis=1)


def halo_x_tracer(block, cells):
    peers = lax.axis_size("gx")
    up = [(peers + i, peers + i + 1) for i in range(peers - 1)]
    down = [(j, i) for i, j in up]
    before = lax.ppermute(block[:, block.shape[1] - cells :], ("half", "gx"), up)
    after = lax.ppermute(block[:, :cells], ("half", "gx"), down)
    return jnp.concatenate([before, block, after], axis=1)


def halo_y(block, rows):
    up, down = shifts("gy")
    below = lax.ppermute(block[:, :, block.shape[2] - rows :], "gy", up)
    above = lax.ppermute(block[:, :, :rows], "gy", down)
    return jnp.concatenate([below, block, above], axis=2)


def to_fine(coarse):
    fields = coarse.shape[0] // 4
    size_x, size_y, depth = (coarse.shape[1], coarse.shape[2], coarse.shape[3])
    split = coarse.reshape(fields, 2, 2, size_x, size_y, depth).transpose(0, 3, 1, 4, 2, 5)
    return split.reshape(fields, 2 * size_x, 2 * size_y, depth)


def to_coarse(fine_cells):
    fields, fine_x, fine_y, depth = fine_cells.shape
    split = fine_cells.reshape(fields, fine_x // 2, 2, fine_y // 2, 2, depth).transpose(
        0, 2, 4, 1, 3, 5
    )
    return split.reshape(fields * 4, fine_x // 2, fine_y // 2, depth)


def fine_levels(levels):
    size_x, size_y = (levels.shape[1], levels.shape[2])
    return (
        levels.reshape(2, 2, size_x, size_y).transpose(2, 0, 3, 1).reshape(2 * size_x, 2 * size_y)
    )


def wet_of(levels, depth):
    shape = levels.shape + (depth,)
    return (lax.broadcasted_iota(jnp.int32, shape, len(shape) - 1) < levels[..., None]).astype(
        jnp.float32
    )


def wet_of_float(levels, depth):
    shape = levels.shape + (depth,)
    return (
        lax.broadcasted_iota(jnp.int32, shape, len(shape) - 1).astype(jnp.float32)
        < levels[..., None]
    ).astype(jnp.float32)


def trim(values, cut, cut_y=None):
    cut_y = cut if cut_y is None else cut_y
    return values[..., cut : values.shape[-3] - cut, cut_y : values.shape[-2] - cut_y, :]


def ocean_substep(fields, wet_mask, heating):
    centre = fields[:, 1:-1, 1:-1]
    to_east = fields[:, 2:, 1:-1]
    to_west = fields[:, :-2, 1:-1]
    to_north = fields[:, 1:-1, 2:]
    to_south = fields[:, 1:-1, :-2]
    speed_east = centre[0]
    speed_north = centre[1]
    advect = speed_east * (to_east - to_west) * 0.5 + speed_north * (to_north - to_south) * 0.5
    spread = to_east + to_west + to_north + to_south - 4.0 * centre
    zeroes = jnp.zeros_like(speed_east)
    forcing = jnp.stack(
        [
            CORIOLIS * speed_north - DRAG * speed_east,
            -CORIOLIS * speed_east - DRAG * speed_north,
            zeroes + heating,
            zeroes,
            zeroes + 1.0,
        ]
    )
    return wet_mask * (centre + DT * (NU * spread - advect + forcing))


def tracer_substep(fields, wet_mask, volume_flux, onehot, eco_rate):
    species = eco_rate.shape[0]
    centre = fields[:, 1:-1, 1:-1]
    to_east = fields[:, 2:, 1:-1]
    to_west = fields[:, :-2, 1:-1]
    to_north = fields[:, 1:-1, 2:]
    to_south = fields[:, 1:-1, :-2]
    advect = (
        volume_flux[0] * (to_east - to_west) * 0.5 + volume_flux[1] * (to_north - to_south) * 0.5
    )
    spread = to_east + to_west + to_north + to_south - 4.0 * centre
    living = centre[:species]
    prey_values = jnp.einsum("ts,sxyk->txyk", onehot, living, precision=lax.Precision.HIGHEST)
    growth = eco_rate[:, None, None, None] * living * jnp.tanh(prey_values) - MORTALITY * living
    reaction = jnp.concatenate([growth, jnp.zeros_like(centre[species:])], axis=0)
    return wet_mask * (centre + DT * (NU * spread - advect + reaction))


def coarse_mean(fine_cells):
    coarse = to_coarse(fine_cells)
    return (
        coarse.reshape(
            fine_cells.shape[0], 4, coarse.shape[1], coarse.shape[2], coarse.shape[3]
        ).sum(axis=1)
        * 0.25
    )


def absorption(tracer, wet_mask, above_table):
    attenuation = wet_mask * (0.03 + 0.05 * jax.nn.softplus(tracer[0]))
    overhead = jnp.einsum("xyk,kl->xyl", attenuation, above_table, precision=lax.Precision.HIGHEST)
    return SURFACE * jnp.exp(-overhead) * (1.0 - jnp.exp(-attenuation))


def body(state, levels, old_flux, eco_prey, eco_rate):
    depth = state.shape[-1]
    size_x, size_y = (state.shape[2], state.shape[3])
    species = eco_rate.shape[0]
    channels = state.shape[1]
    is_ocean = lax.axis_index("half") == 0
    level_lanes = jnp.pad(
        levels.astype(jnp.float32).transpose(1, 2, 0), ((0, 0), (0, 0), (0, depth - 4))
    )[None]
    packed = jnp.concatenate([state[0], old_flux, level_lanes], axis=0)
    reach_x, reach_y = size_x, NSUB + 1
    ext1 = halo_y(halo_x(packed, reach_x), reach_y)
    onehot = (eco_prey[:, None] == lax.broadcasted_iota(jnp.int32, (species, species), 1)).astype(
        jnp.float32
    )
    above_table = (
        lax.broadcasted_iota(jnp.int32, (depth, depth), 0)
        < lax.broadcasted_iota(jnp.int32, (depth, depth), 1)
    ).astype(jnp.float32)
    wet_fine = wet_of(fine_levels(levels), depth)
    wet_coarse = wet_of(jnp.max(levels, axis=0), depth)
    raw_ext = ext1[:channels]
    flux_ext = ext1[channels : channels + 2]
    levels_ext = ext1[channels + 2, :, :, 0:4].transpose(2, 0, 1)
    wet_coarse_ext = wet_of_float(jnp.max(levels_ext, axis=0), depth)
    wet_fine_ext = wet_of_float(fine_levels(levels_ext), depth)
    zeros_flux = jnp.zeros((2, size_x, size_y, depth), jnp.float32)
    mid_y, late_y = reach_y - 2, reach_y - 4
    shape_mid = (channels, size_x, size_y + 2 * mid_y, depth)
    shape_late = (channels, size_x, size_y + 2 * late_y, depth)

    def ocean_a():
        cut = 2 * reach_y - 2 * mid_y - 2
        fine = trim(to_fine(raw_ext) * wet_fine_ext[None], 2 * reach_x - 2, cut)
        running = zeros_flux
        for substep in range(2):
            fine = ocean_substep(
                fine, trim(wet_fine_ext, 2 * reach_x - 1 + substep, cut + substep + 1), 0.0
            )
            running = running + coarse_mean(trim(fine[0:2], 1 - substep, 2 * mid_y + 1 - substep))
        return to_coarse(fine), running

    def tracer_a():
        tracer = raw_ext * wet_coarse_ext[None]
        for substep in range(2):
            tracer = tracer_substep(
                tracer,
                trim(wet_coarse_ext, substep + 1),
                trim(flux_ext, substep + 1),
                onehot,
                eco_rate,
            )
        return tracer, zeros_flux

    block_mid, running = lax.cond(is_ocean, ocean_a, tracer_a)
    ext2 = halo_x(block_mid, reach_x)
    fine_shape = (channels // 4, 2 * size_x + 2, 2 * size_y + 2, depth)

    def ocean_b():
        fine = trim(to_fine(ext2), 2 * reach_x - 3, 2 * mid_y - 3)
        summed = running
        for substep in range(2):
            fine = ocean_substep(
                fine, trim(wet_fine_ext, 2 * reach_x - 2 + substep, 2 * reach_y - 2 + substep), 0.0
            )
            summed = summed + coarse_mean(trim(fine[0:2], 2 - substep))
        return jnp.zeros(shape_late, jnp.float32), fine, summed / NSUB

    def tracer_b():
        tracer = ext2
        for substep in range(2):
            tracer = tracer_substep(
                tracer,
                trim(wet_coarse_ext, substep + 1, reach_y - mid_y + substep + 1),
                trim(flux_ext, substep + 1, reach_y - mid_y + substep + 1),
                onehot,
                eco_rate,
            )
        absorbed = absorption(trim(tracer, 0, late_y), wet_coarse, above_table)
        outgoing = jnp.broadcast_to(absorbed[None], (2, size_x, size_y, depth))
        return tracer, jnp.zeros(fine_shape, jnp.float32), outgoing

    block_late, ocean_late, outgoing = lax.cond(is_ocean, ocean_b, tracer_b)
    ext3 = halo_x_tracer(block_late, 1)
    arrived = lax.ppermute(outgoing, "half", [(0, 1), (1, 0)])

    def ocean_c():
        light = arrived[0:1]
        heating = HEATING * to_fine(jnp.broadcast_to(light, (4, size_x, size_y, depth)))[0]
        return to_coarse(ocean_substep(ocean_late, wet_fine, heating))

    def tracer_c():
        return tracer_substep(trim(ext3, 0, late_y - 1), wet_coarse, arrived, onehot, eco_rate)

    return lax.cond(is_ocean, ocean_c, tracer_c)[None]


def solution(mesh):
    placed = (
        P("half", None, "gx", "gy", None),
        P(None, "gx", "gy"),
        P(None, "gx", "gy", None),
        P(),
        P(),
    )
    return jax.shard_map(
        body,
        mesh=mesh,
        in_specs=placed,
        out_specs=P("half", None, "gx", "gy", None),
        check_vma=False,
    )
```

```python
import jax
import jax.numpy as jnp
from jax import lax
from jax.sharding import PartitionSpec as P

NSUB = 4


DT = 0.1
NU = 1.0
CORIOLIS = 0.5
DRAG = 0.1
MORTALITY = 0.1
HEATING = 2.0
SURFACE = 8.0


def shifts(axis):
    peers = lax.axis_size(axis)
    up = [(i, i + 1) for i in range(peers - 1)]
    down = [(j, i) for i, j in up]
    return up, down


def halo_x(block, cells):
    up, down = shifts("gx")
    before = lax.ppermute(block[:, block.shape[1] - cells :], "gx", up)
    after = lax.ppermute(block[:, :cells], "gx", down)
    return jnp.concatenate([before, block, after], axis=1)


def halo_x_tracer(block, cells):
    peers = lax.axis_size("gx")
    up = [(peers + i, peers + i + 1) for i in range(peers - 1)]
    down = [(j, i) for i, j in up]
    before = lax.ppermute(block[:, block.shape[1] - cells :], ("half", "gx"), up)
    after = lax.ppermute(block[:, :cells], ("half", "gx"), down)
    return jnp.concatenate([before, block, after], axis=1)


def halo_y(block, rows):
    up, down = shifts("gy")
    below = lax.ppermute(block[:, :, block.shape[2] - rows :], "gy", up)
    above = lax.ppermute(block[:, :, :rows], "gy", down)
    return jnp.concatenate([below, block, above], axis=2)


def to_fine(coarse):
    fields = coarse.shape[0] // 4
    size_x, size_y, depth = (coarse.shape[1], coarse.shape[2], coarse.shape[3])
    split = coarse.reshape(fields, 2, 2, size_x, size_y, depth).transpose(0, 3, 1, 4, 2, 5)
    return split.reshape(fields, 2 * size_x, 2 * size_y, depth)


def to_coarse(fine_cells):
    fields, fine_x, fine_y, depth = fine_cells.shape
    split = fine_cells.reshape(fields, fine_x // 2, 2, fine_y // 2, 2, depth).transpose(
        0, 2, 4, 1, 3, 5
    )
    return split.reshape(fields * 4, fine_x // 2, fine_y // 2, depth)


def fine_levels(levels):
    size_x, size_y = (levels.shape[1], levels.shape[2])
    return (
        levels.reshape(2, 2, size_x, size_y).transpose(2, 0, 3, 1).reshape(2 * size_x, 2 * size_y)
    )


def wet_of(levels, depth):
    shape = levels.shape + (depth,)
    return (lax.broadcasted_iota(jnp.int32, shape, len(shape) - 1) < levels[..., None]).astype(
        jnp.float32
    )


def wet_of_float(levels, depth):
    shape = levels.shape + (depth,)
    return (
        lax.broadcasted_iota(jnp.int32, shape, len(shape) - 1).astype(jnp.float32)
        < levels[..., None]
    ).astype(jnp.float32)


def trim(values, cut, cut_y=None):
    cut_y = cut if cut_y is None else cut_y
    return values[..., cut : values.shape[-3] - cut, cut_y : values.shape[-2] - cut_y, :]


def ocean_substep(fields, wet_mask, heating):
    centre = fields[:, 1:-1, 1:-1]
    to_east = fields[:, 2:, 1:-1]
    to_west = fields[:, :-2, 1:-1]
    to_north = fields[:, 1:-1, 2:]
    to_south = fields[:, 1:-1, :-2]
    speed_east = centre[0]
    speed_north = centre[1]
    advect = speed_east * (to_east - to_west) * 0.5 + speed_north * (to_north - to_south) * 0.5
    spread = to_east + to_west + to_north + to_south - 4.0 * centre
    zeroes = jnp.zeros_like(speed_east)
    forcing = jnp.stack(
        [
            CORIOLIS * speed_north - DRAG * speed_east,
            -CORIOLIS * speed_east - DRAG * speed_north,
            zeroes + heating,
            zeroes,
            zeroes + 1.0,
        ]
    )
    return wet_mask * (centre + DT * (NU * spread - advect + forcing))


def tracer_substep(fields, wet_mask, volume_flux, onehot, eco_rate):
    species = eco_rate.shape[0]
    centre = fields[:, 1:-1, 1:-1]
    to_east = fields[:, 2:, 1:-1]
    to_west = fields[:, :-2, 1:-1]
    to_north = fields[:, 1:-1, 2:]
    to_south = fields[:, 1:-1, :-2]
    advect = (
        volume_flux[0] * (to_east - to_west) * 0.5 + volume_flux[1] * (to_north - to_south) * 0.5
    )
    spread = to_east + to_west + to_north + to_south - 4.0 * centre
    living = centre[:species]
    prey_values = jnp.einsum("ts,sxyk->txyk", onehot, living, precision=lax.Precision.HIGHEST)
    growth = eco_rate[:, None, None, None] * living * jnp.tanh(prey_values) - MORTALITY * living
    reaction = jnp.concatenate([growth, jnp.zeros_like(centre[species:])], axis=0)
    return wet_mask * (centre + DT * (NU * spread - advect + reaction))


def coarse_mean(fine_cells):
    coarse = to_coarse(fine_cells)
    return (
        coarse.reshape(
            fine_cells.shape[0], 4, coarse.shape[1], coarse.shape[2], coarse.shape[3]
        ).sum(axis=1)
        * 0.25
    )


def absorption(tracer, wet_mask, above_table):
    attenuation = wet_mask * (0.03 + 0.05 * jax.nn.softplus(tracer[0]))
    overhead = jnp.einsum("xyk,kl->xyl", attenuation, above_table, precision=lax.Precision.HIGHEST)
    return SURFACE * jnp.exp(-overhead) * (1.0 - jnp.exp(-attenuation))


def body(state, levels, old_flux, eco_prey, eco_rate):
    depth = state.shape[-1]
    size_x, size_y = (state.shape[2], state.shape[3])
    species = eco_rate.shape[0]
    channels = state.shape[1]
    is_ocean = lax.axis_index("half") == 0
    level_lanes = jnp.pad(
        levels.astype(jnp.float32).transpose(1, 2, 0), ((0, 0), (0, 0), (0, depth - 4))
    )[None]
    packed = jnp.concatenate([state[0], old_flux, level_lanes], axis=0)
    reach_x, reach_y = size_x, NSUB + 1
    ext1 = halo_y(halo_x(packed, reach_x), reach_y)
    onehot = (eco_prey[:, None] == lax.broadcasted_iota(jnp.int32, (species, species), 1)).astype(
        jnp.float32
    )
    above_table = (
        lax.broadcasted_iota(jnp.int32, (depth, depth), 0)
        < lax.broadcasted_iota(jnp.int32, (depth, depth), 1)
    ).astype(jnp.float32)
    wet_fine = wet_of(fine_levels(levels), depth)
    wet_coarse = wet_of(jnp.max(levels, axis=0), depth)
    raw_ext = ext1[:channels]
    flux_ext = ext1[channels : channels + 2]
    levels_ext = ext1[channels + 2, :, :, 0:4].transpose(2, 0, 1)
    wet_coarse_ext = wet_of_float(jnp.max(levels_ext, axis=0), depth)
    wet_fine_ext = wet_of_float(fine_levels(levels_ext), depth)
    zeros_flux = jnp.zeros((2, size_x, size_y, depth), jnp.float32)
    mid_y, late_y = reach_y - 2, reach_y - 4
    shape_mid = (channels, size_x, size_y + 2 * mid_y, depth)
    shape_late = (channels, size_x, size_y + 2 * late_y, depth)

    def ocean_a():
        cut = 2 * reach_y - 2 * mid_y - 2
        fine = trim(to_fine(raw_ext) * wet_fine_ext[None], 2 * reach_x - 2, cut)
        running = zeros_flux
        for substep in range(2):
            fine = ocean_substep(
                fine, trim(wet_fine_ext, 2 * reach_x - 1 + substep, cut + substep + 1), 0.0
            )
            running = running + coarse_mean(trim(fine[0:2], 1 - substep, 2 * mid_y + 1 - substep))
        return to_coarse(fine), running

    def tracer_a():
        tracer = raw_ext * wet_coarse_ext[None]
        for substep in range(2):
            tracer = tracer_substep(
                tracer,
                trim(wet_coarse_ext, substep + 1),
                trim(flux_ext, substep + 1),
                onehot,
                eco_rate,
            )
        return tracer, zeros_flux

    block_mid, running = lax.cond(is_ocean, ocean_a, tracer_a)
    ext2 = halo_x(block_mid, reach_x)
    fine_shape = (channels // 4, 2 * size_x + 2, 2 * size_y + 2, depth)

    def ocean_b():
        fine = trim(to_fine(ext2), 2 * reach_x - 3, 2 * mid_y - 3)
        summed = running
        for substep in range(2):
            fine = ocean_substep(
                fine, trim(wet_fine_ext, 2 * reach_x - 2 + substep, 2 * reach_y - 2 + substep), 0.0
            )
            summed = summed + coarse_mean(trim(fine[0:2], 2 - substep))
        return jnp.zeros(shape_late, jnp.float32), fine, summed

    def tracer_b():
        tracer = ext2
        for substep in range(2):
            tracer = tracer_substep(
                tracer,
                trim(wet_coarse_ext, substep + 1, reach_y - mid_y + substep + 1),
                trim(flux_ext, substep + 1, reach_y - mid_y + substep + 1),
                onehot,
                eco_rate,
            )
        return tracer, jnp.zeros(fine_shape, jnp.float32), running

    block_late, ocean_late, summed = lax.cond(is_ocean, ocean_b, tracer_b)
    ext3 = halo_x_tracer(block_late, 1)

    def tracer_light():
        absorbed = absorption(trim(block_late, 0, late_y), wet_coarse, above_table)
        return jnp.broadcast_to(absorbed[None], (2, size_x, size_y, depth))

    outgoing = lax.cond(is_ocean, lambda: summed / NSUB, tracer_light)
    outgoing, ext3 = lax.optimization_barrier((outgoing, ext3))
    arrived = lax.ppermute(outgoing, "half", [(0, 1), (1, 0)])

    def ocean_c():
        light = arrived[0:1]
        heating = HEATING * to_fine(jnp.broadcast_to(light, (4, size_x, size_y, depth)))[0]
        return to_coarse(ocean_substep(ocean_late, wet_fine, heating))

    def tracer_c():
        return tracer_substep(trim(ext3, 0, late_y - 1), wet_coarse, arrived, onehot, eco_rate)

    return lax.cond(is_ocean, ocean_c, tracer_c)[None]


def solution(mesh):
    placed = (
        P("half", None, "gx", "gy", None),
        P(None, "gx", "gy"),
        P(None, "gx", "gy", None),
        P(),
        P(),
    )
    return jax.shard_map(
        body,
        mesh=mesh,
        in_specs=placed,
        out_specs=P("half", None, "gx", "gy", None),
        check_vma=False,
    )
```

```python
import jax
import jax.numpy as jnp
from jax import lax
from jax.sharding import PartitionSpec as P

NSUB = 4


DT = 0.1
NU = 1.0
CORIOLIS = 0.5
DRAG = 0.1
MORTALITY = 0.1
HEATING = 2.0
SURFACE = 8.0


def shifts(axis):
    peers = lax.axis_size(axis)
    up = [(i, i + 1) for i in range(peers - 1)]
    down = [(j, i) for i, j in up]
    return up, down


def halo_x(block, cells):
    up, down = shifts("gx")
    before = lax.ppermute(block[:, block.shape[1] - cells :], "gx", up)
    after = lax.ppermute(block[:, :cells], "gx", down)
    return jnp.concatenate([before, block, after], axis=1)


def halo_x_tracer(block, cells):
    peers = lax.axis_size("gx")
    up = [(peers + i, peers + i + 1) for i in range(peers - 1)]
    down = [(j, i) for i, j in up]
    before = lax.ppermute(block[:, block.shape[1] - cells :], ("half", "gx"), up)
    after = lax.ppermute(block[:, :cells], ("half", "gx"), down)
    return jnp.concatenate([before, block, after], axis=1)


def halo_y(block, rows):
    up, down = shifts("gy")
    below = lax.ppermute(block[:, :, block.shape[2] - rows :], "gy", up)
    above = lax.ppermute(block[:, :, :rows], "gy", down)
    return jnp.concatenate([below, block, above], axis=2)


def to_fine(coarse):
    fields = coarse.shape[0] // 4
    size_x, size_y, depth = (coarse.shape[1], coarse.shape[2], coarse.shape[3])
    split = coarse.reshape(fields, 2, 2, size_x, size_y, depth).transpose(0, 3, 1, 4, 2, 5)
    return split.reshape(fields, 2 * size_x, 2 * size_y, depth)


def to_coarse(fine_cells):
    fields, fine_x, fine_y, depth = fine_cells.shape
    split = fine_cells.reshape(fields, fine_x // 2, 2, fine_y // 2, 2, depth).transpose(
        0, 2, 4, 1, 3, 5
    )
    return split.reshape(fields * 4, fine_x // 2, fine_y // 2, depth)


def fine_levels(levels):
    size_x, size_y = (levels.shape[1], levels.shape[2])
    return (
        levels.reshape(2, 2, size_x, size_y).transpose(2, 0, 3, 1).reshape(2 * size_x, 2 * size_y)
    )


def wet_of(levels, depth):
    shape = levels.shape + (depth,)
    return (lax.broadcasted_iota(jnp.int32, shape, len(shape) - 1) < levels[..., None]).astype(
        jnp.float32
    )


def wet_of_float(levels, depth):
    shape = levels.shape + (depth,)
    return (
        lax.broadcasted_iota(jnp.int32, shape, len(shape) - 1).astype(jnp.float32)
        < levels[..., None]
    ).astype(jnp.float32)


def trim(values, cut, cut_y=None):
    cut_y = cut if cut_y is None else cut_y
    return values[..., cut : values.shape[-3] - cut, cut_y : values.shape[-2] - cut_y, :]


def ocean_substep(fields, wet_mask, heating):
    centre = fields[:, 1:-1, 1:-1]
    to_east = fields[:, 2:, 1:-1]
    to_west = fields[:, :-2, 1:-1]
    to_north = fields[:, 1:-1, 2:]
    to_south = fields[:, 1:-1, :-2]
    speed_east = centre[0]
    speed_north = centre[1]
    advect = speed_east * (to_east - to_west) * 0.5 + speed_north * (to_north - to_south) * 0.5
    spread = to_east + to_west + to_north + to_south - 4.0 * centre
    zeroes = jnp.zeros_like(speed_east)
    forcing = jnp.stack(
        [
            CORIOLIS * speed_north - DRAG * speed_east,
            -CORIOLIS * speed_east - DRAG * speed_north,
            zeroes + heating,
            zeroes,
            zeroes + 1.0,
        ]
    )
    return wet_mask * (centre + DT * (NU * spread - advect + forcing))


def ocean_substep_channels(fields, wet_mask, heating):
    pad = ((0, 0), (0, 0), (0, 0), (1, 1), (1, 1), (0, 0))
    wide = jnp.pad(fields, pad)
    to_east = jnp.concatenate([fields[:, 1:2], wide[:, 0:1, :, 2:, 1:-1]], axis=1)
    to_west = jnp.concatenate([wide[:, 1:2, :, :-2, 1:-1], fields[:, 0:1]], axis=1)
    to_north = jnp.concatenate([fields[:, :, 1:2], wide[:, :, 0:1, 1:-1, 2:]], axis=2)
    to_south = jnp.concatenate([wide[:, :, 1:2, 1:-1, :-2], fields[:, :, 0:1]], axis=2)
    centre = fields
    speed_east = centre[0]
    speed_north = centre[1]
    advect = speed_east * (to_east - to_west) * 0.5 + speed_north * (to_north - to_south) * 0.5
    spread = to_east + to_west + to_north + to_south - 4.0 * centre
    zeroes = jnp.zeros_like(speed_east)
    forcing = jnp.stack(
        [
            CORIOLIS * speed_north - DRAG * speed_east,
            -CORIOLIS * speed_east - DRAG * speed_north,
            zeroes + heating,
            zeroes,
            zeroes + 1.0,
        ]
    )
    return wet_mask * (centre + DT * (NU * spread - advect + forcing))


def channel_mean(fields):
    coarse = fields.reshape((fields.shape[0], 4) + fields.shape[3:])
    return coarse.sum(axis=1) * 0.25


def tracer_substep(fields, wet_mask, volume_flux, onehot, eco_rate):
    species = eco_rate.shape[0]
    centre = fields[:, 1:-1, 1:-1]
    to_east = fields[:, 2:, 1:-1]
    to_west = fields[:, :-2, 1:-1]
    to_north = fields[:, 1:-1, 2:]
    to_south = fields[:, 1:-1, :-2]
    advect = (
        volume_flux[0] * (to_east - to_west) * 0.5 + volume_flux[1] * (to_north - to_south) * 0.5
    )
    spread = to_east + to_west + to_north + to_south - 4.0 * centre
    living = centre[:species]
    prey_values = jnp.einsum("ts,sxyk->txyk", onehot, living, precision=lax.Precision.HIGHEST)
    growth = eco_rate[:, None, None, None] * living * jnp.tanh(prey_values) - MORTALITY * living
    reaction = jnp.concatenate([growth, jnp.zeros_like(centre[species:])], axis=0)
    return wet_mask * (centre + DT * (NU * spread - advect + reaction))


def coarse_mean(fine_cells):
    coarse = to_coarse(fine_cells)
    return (
        coarse.reshape(
            fine_cells.shape[0], 4, coarse.shape[1], coarse.shape[2], coarse.shape[3]
        ).sum(axis=1)
        * 0.25
    )


def absorption(tracer, wet_mask, above_table):
    attenuation = wet_mask * (0.03 + 0.05 * jax.nn.softplus(tracer[0]))
    overhead = jnp.einsum("xyk,kl->xyl", attenuation, above_table, precision=lax.Precision.HIGHEST)
    return SURFACE * jnp.exp(-overhead) * (1.0 - jnp.exp(-attenuation))


def body(state, levels, old_flux, eco_prey, eco_rate):
    depth = state.shape[-1]
    size_x, size_y = (state.shape[2], state.shape[3])
    species = eco_rate.shape[0]
    channels = state.shape[1]
    is_ocean = lax.axis_index("half") == 0
    level_lanes = jnp.pad(
        levels.astype(jnp.float32).transpose(1, 2, 0), ((0, 0), (0, 0), (0, depth - 4))
    )[None]
    packed = jnp.concatenate([state[0], old_flux, level_lanes], axis=0)
    reach_x, reach_y = size_x, NSUB + 1
    ext1 = halo_y(halo_x(packed, reach_x), reach_y)
    onehot = (eco_prey[:, None] == lax.broadcasted_iota(jnp.int32, (species, species), 1)).astype(
        jnp.float32
    )
    above_table = (
        lax.broadcasted_iota(jnp.int32, (depth, depth), 0)
        < lax.broadcasted_iota(jnp.int32, (depth, depth), 1)
    ).astype(jnp.float32)
    wet_coarse = wet_of(jnp.max(levels, axis=0), depth)
    raw_ext = ext1[:channels]
    flux_ext = ext1[channels : channels + 2]
    levels_ext = ext1[channels + 2, :, :, 0:4].transpose(2, 0, 1)
    wet_coarse_ext = wet_of_float(jnp.max(levels_ext, axis=0), depth)
    zeros_flux = jnp.zeros((2, size_x, size_y, depth), jnp.float32)
    mid_y, late_y = reach_y - 2, reach_y - 4
    shape_mid = (channels, size_x, size_y + 2 * mid_y, depth)
    shape_late = (channels, size_x, size_y + 2 * late_y, depth)

    wet_ch_ext = wet_of_float(levels_ext, depth).reshape((2, 2) + levels_ext.shape[1:] + (depth,))

    def as_fields(block):
        return block.reshape((channels // 4, 2, 2) + block.shape[1:])

    def ocean_a():
        fields = as_fields(raw_ext)[..., 1:-1, 1:-1, :]
        wet = wet_ch_ext[..., 1:-1, 1:-1, :]
        fields = fields * wet[None]
        running = zeros_flux
        for substep in range(2):
            fields = ocean_substep_channels(fields, wet, 0.0)
            running = running + channel_mean(
                fields[0:2, :, :, 1 : 1 + size_x, reach_y - 1 : reach_y - 1 + size_y]
            )
        keep = fields[..., 1 : 1 + size_x, reach_y - 1 - mid_y : reach_y - 1 + size_y + mid_y, :]
        return keep.reshape(shape_mid), running

    def tracer_a():
        tracer = raw_ext * wet_coarse_ext[None]
        for substep in range(2):
            tracer = tracer_substep(
                tracer,
                trim(wet_coarse_ext, substep + 1),
                trim(flux_ext, substep + 1),
                onehot,
                eco_rate,
            )
        return tracer, zeros_flux

    block_mid, running = lax.cond(is_ocean, ocean_a, tracer_a)
    ext2 = halo_x(block_mid, reach_x)
    fine_shape = (channels // 4, 2 * size_x + 2, 2 * size_y + 2, depth)

    fine_shape = (channels, size_x + 2, size_y + 2, depth)

    def ocean_b():
        cut_y = mid_y - 2
        fields = as_fields(ext2)[..., cut_y : ext2.shape[2] - cut_y, :]
        wet = wet_ch_ext[..., reach_x - 2 : wet_ch_ext.shape[2] - reach_x + 2, reach_y - 2 : wet_ch_ext.shape[3] - reach_y + 2, :]
        summed = running
        for substep in range(2):
            fields = ocean_substep_channels(fields, wet, 0.0)
            summed = summed + channel_mean(fields[0:2, :, :, 2 : 2 + size_x, 2 : 2 + size_y])
        keep = fields[..., 1:-1, 1:-1, :]
        return jnp.zeros(shape_late, jnp.float32), keep.reshape(fine_shape), summed / NSUB

    def tracer_b():
        tracer = ext2
        for substep in range(2):
            tracer = tracer_substep(
                tracer,
                trim(wet_coarse_ext, substep + 1, reach_y - mid_y + substep + 1),
                trim(flux_ext, substep + 1, reach_y - mid_y + substep + 1),
                onehot,
                eco_rate,
            )
        absorbed = absorption(trim(tracer, 0, late_y), wet_coarse, above_table)
        outgoing = jnp.broadcast_to(absorbed[None], (2, size_x, size_y, depth))
        return tracer, jnp.zeros(fine_shape, jnp.float32), outgoing

    block_late, ocean_late, outgoing = lax.cond(is_ocean, ocean_b, tracer_b)
    ext3 = halo_x_tracer(block_late, 1)
    arrived = lax.ppermute(outgoing, "half", [(0, 1), (1, 0)])

    def ocean_c():
        light = jnp.pad(arrived[0], ((1, 1), (1, 1), (0, 0)))
        heating = HEATING * jnp.broadcast_to(light, (2, 2) + light.shape)
        wet = wet_ch_ext[..., reach_x - 1 : wet_ch_ext.shape[2] - reach_x + 1, reach_y - 1 : wet_ch_ext.shape[3] - reach_y + 1, :]
        fields = ocean_substep_channels(as_fields(ocean_late), wet, heating)
        return fields[..., 1 : 1 + size_x, 1 : 1 + size_y, :].reshape(channels, size_x, size_y, depth)

    def tracer_c():
        return tracer_substep(trim(ext3, 0, late_y - 1), wet_coarse, arrived, onehot, eco_rate)

    return lax.cond(is_ocean, ocean_c, tracer_c)[None]


def solution(mesh):
    placed = (
        P("half", None, "gx", "gy", None),
        P(None, "gx", "gy"),
        P(None, "gx", "gy", None),
        P(),
        P(),
    )
    return jax.shard_map(
        body,
        mesh=mesh,
        in_specs=placed,
        out_specs=P("half", None, "gx", "gy", None),
        check_vma=False,
    )
```

```python
import jax
import jax.numpy as jnp
from jax import lax
from jax.sharding import PartitionSpec as P

NSUB = 4


DT = 0.1
NU = 1.0
CORIOLIS = 0.5
DRAG = 0.1
MORTALITY = 0.1
HEATING = 2.0
SURFACE = 8.0


def shifts(axis):
    peers = lax.axis_size(axis)
    up = [(i, i + 1) for i in range(peers - 1)]
    down = [(j, i) for i, j in up]
    return up, down


def halo_x(block, cells):
    up, down = shifts("gx")
    before = lax.ppermute(block[:, block.shape[1] - cells :], "gx", up)
    after = lax.ppermute(block[:, :cells], "gx", down)
    return jnp.concatenate([before, block, after], axis=1)


def halo_x_tracer(block, cells):
    peers = lax.axis_size("gx")
    up = [(peers + i, peers + i + 1) for i in range(peers - 1)]
    down = [(j, i) for i, j in up]
    before = lax.ppermute(block[:, block.shape[1] - cells :], ("half", "gx"), up)
    after = lax.ppermute(block[:, :cells], ("half", "gx"), down)
    return jnp.concatenate([before, block, after], axis=1)


def halo_y(block, rows):
    up, down = shifts("gy")
    below = lax.ppermute(block[:, :, block.shape[2] - rows :], "gy", up)
    above = lax.ppermute(block[:, :, :rows], "gy", down)
    return jnp.concatenate([below, block, above], axis=2)


def to_fine(coarse):
    fields = coarse.shape[0] // 4
    size_x, size_y, depth = (coarse.shape[1], coarse.shape[2], coarse.shape[3])
    split = coarse.reshape(fields, 2, 2, size_x, size_y, depth).transpose(0, 3, 1, 4, 2, 5)
    return split.reshape(fields, 2 * size_x, 2 * size_y, depth)


def to_coarse(fine_cells):
    fields, fine_x, fine_y, depth = fine_cells.shape
    split = fine_cells.reshape(fields, fine_x // 2, 2, fine_y // 2, 2, depth).transpose(
        0, 2, 4, 1, 3, 5
    )
    return split.reshape(fields * 4, fine_x // 2, fine_y // 2, depth)


def fine_levels(levels):
    size_x, size_y = (levels.shape[1], levels.shape[2])
    return (
        levels.reshape(2, 2, size_x, size_y).transpose(2, 0, 3, 1).reshape(2 * size_x, 2 * size_y)
    )


def wet_of(levels, depth):
    shape = levels.shape + (depth,)
    return (lax.broadcasted_iota(jnp.int32, shape, len(shape) - 1) < levels[..., None]).astype(
        jnp.float32
    )


def wet_of_float(levels, depth):
    shape = levels.shape + (depth,)
    return (
        lax.broadcasted_iota(jnp.int32, shape, len(shape) - 1).astype(jnp.float32)
        < levels[..., None]
    ).astype(jnp.float32)


def trim(values, cut, cut_y=None):
    cut_y = cut if cut_y is None else cut_y
    return values[..., cut : values.shape[-3] - cut, cut_y : values.shape[-2] - cut_y, :]


def ocean_substep(fields, wet_mask, heating):
    centre = fields[:, 1:-1, 1:-1]
    to_east = fields[:, 2:, 1:-1]
    to_west = fields[:, :-2, 1:-1]
    to_north = fields[:, 1:-1, 2:]
    to_south = fields[:, 1:-1, :-2]
    speed_east = centre[0]
    speed_north = centre[1]
    advect = speed_east * (to_east - to_west) * 0.5 + speed_north * (to_north - to_south) * 0.5
    spread = to_east + to_west + to_north + to_south - 4.0 * centre
    zeroes = jnp.zeros_like(speed_east)
    forcing = jnp.stack(
        [
            CORIOLIS * speed_north - DRAG * speed_east,
            -CORIOLIS * speed_east - DRAG * speed_north,
            zeroes + heating,
            zeroes,
            zeroes + 1.0,
        ]
    )
    return wet_mask * (centre + DT * (NU * spread - advect + forcing))


def ocean_substep_channels(fields, wet_mask, heating):
    pad = ((0, 0), (0, 0), (0, 0), (1, 1), (1, 1), (0, 0))
    wide = jnp.pad(fields, pad)
    to_east = jnp.concatenate([fields[:, 1:2], wide[:, 0:1, :, 2:, 1:-1]], axis=1)
    to_west = jnp.concatenate([wide[:, 1:2, :, :-2, 1:-1], fields[:, 0:1]], axis=1)
    to_north = jnp.concatenate([fields[:, :, 1:2], wide[:, :, 0:1, 1:-1, 2:]], axis=2)
    to_south = jnp.concatenate([wide[:, :, 1:2, 1:-1, :-2], fields[:, :, 0:1]], axis=2)
    centre = fields
    speed_east = centre[0]
    speed_north = centre[1]
    advect = speed_east * (to_east - to_west) * 0.5 + speed_north * (to_north - to_south) * 0.5
    spread = to_east + to_west + to_north + to_south - 4.0 * centre
    zeroes = jnp.zeros_like(speed_east)
    forcing = jnp.stack(
        [
            CORIOLIS * speed_north - DRAG * speed_east,
            -CORIOLIS * speed_east - DRAG * speed_north,
            zeroes + heating,
            zeroes,
            zeroes + 1.0,
        ]
    )
    return wet_mask * (centre + DT * (NU * spread - advect + forcing))


def channel_mean(fields):
    coarse = fields.reshape((fields.shape[0], 4) + fields.shape[3:])
    return coarse.sum(axis=1) * 0.25


def tracer_substep(fields, wet_mask, volume_flux, onehot, eco_rate):
    species = eco_rate.shape[0]
    centre = fields[:, 1:-1, 1:-1]
    to_east = fields[:, 2:, 1:-1]
    to_west = fields[:, :-2, 1:-1]
    to_north = fields[:, 1:-1, 2:]
    to_south = fields[:, 1:-1, :-2]
    advect = (
        volume_flux[0] * (to_east - to_west) * 0.5 + volume_flux[1] * (to_north - to_south) * 0.5
    )
    spread = to_east + to_west + to_north + to_south - 4.0 * centre
    living = centre[:species]
    prey_values = jnp.take(living, onehot, axis=0)
    growth = eco_rate[:, None, None, None] * living * jnp.tanh(prey_values) - MORTALITY * living
    reaction = jnp.concatenate([growth, jnp.zeros_like(centre[species:])], axis=0)
    return wet_mask * (centre + DT * (NU * spread - advect + reaction))


def coarse_mean(fine_cells):
    coarse = to_coarse(fine_cells)
    return (
        coarse.reshape(
            fine_cells.shape[0], 4, coarse.shape[1], coarse.shape[2], coarse.shape[3]
        ).sum(axis=1)
        * 0.25
    )


def absorption(tracer, wet_mask, above_table):
    attenuation = wet_mask * (0.03 + 0.05 * jax.nn.softplus(tracer[0]))
    overhead = jnp.einsum("xyk,kl->xyl", attenuation, above_table, precision=lax.Precision.HIGHEST)
    return SURFACE * jnp.exp(-overhead) * (1.0 - jnp.exp(-attenuation))


def body(state, levels, old_flux, eco_prey, eco_rate):
    depth = state.shape[-1]
    size_x, size_y = (state.shape[2], state.shape[3])
    species = eco_rate.shape[0]
    channels = state.shape[1]
    is_ocean = lax.axis_index("half") == 0
    level_lanes = jnp.pad(
        levels.astype(jnp.float32).transpose(1, 2, 0), ((0, 0), (0, 0), (0, depth - 4))
    )[None]
    packed = jnp.concatenate([state[0], old_flux, level_lanes], axis=0)
    reach_x, reach_y = size_x, NSUB + 1
    ext1 = halo_y(halo_x(packed, reach_x), reach_y)
    onehot = jnp.clip(eco_prey, 0, species - 1)
    above_table = (
        lax.broadcasted_iota(jnp.int32, (depth, depth), 0)
        < lax.broadcasted_iota(jnp.int32, (depth, depth), 1)
    ).astype(jnp.float32)
    wet_coarse = wet_of(jnp.max(levels, axis=0), depth)
    raw_ext = ext1[:channels]
    flux_ext = ext1[channels : channels + 2]
    levels_ext = ext1[channels + 2, :, :, 0:4].transpose(2, 0, 1)
    wet_coarse_ext = wet_of_float(jnp.max(levels_ext, axis=0), depth)
    zeros_flux = jnp.zeros((2, size_x, size_y, depth), jnp.float32)
    mid_y, late_y = reach_y - 2, reach_y - 4
    shape_mid = (channels, size_x, size_y + 2 * mid_y, depth)
    shape_late = (channels, size_x, size_y + 2 * late_y, depth)

    wet_ch_ext = wet_of_float(levels_ext, depth).reshape((2, 2) + levels_ext.shape[1:] + (depth,))

    def as_fields(block):
        return block.reshape((channels // 4, 2, 2) + block.shape[1:])

    def ocean_a():
        fields = as_fields(raw_ext)[..., 1:-1, 1:-1, :]
        wet = wet_ch_ext[..., 1:-1, 1:-1, :]
        fields = fields * wet[None]
        running = zeros_flux
        for substep in range(2):
            fields = ocean_substep_channels(fields, wet, 0.0)
            running = running + channel_mean(
                fields[0:2, :, :, 1 : 1 + size_x, reach_y - 1 : reach_y - 1 + size_y]
            )
        keep = fields[..., 1 : 1 + size_x, reach_y - 1 - mid_y : reach_y - 1 + size_y + mid_y, :]
        return keep.reshape(shape_mid), running

    def tracer_a():
        tracer = raw_ext * wet_coarse_ext[None]
        for substep in range(2):
            tracer = tracer_substep(
                tracer,
                trim(wet_coarse_ext, substep + 1),
                trim(flux_ext, substep + 1),
                onehot,
                eco_rate,
            )
        return tracer, zeros_flux

    block_mid, running = lax.cond(is_ocean, ocean_a, tracer_a)
    ext2 = halo_x(block_mid, reach_x)
    fine_shape = (channels // 4, 2 * size_x + 2, 2 * size_y + 2, depth)

    fine_shape = (channels, size_x + 2, size_y + 2, depth)

    def ocean_b():
        cut_y = mid_y - 2
        fields = as_fields(ext2)[..., cut_y : ext2.shape[2] - cut_y, :]
        wet = wet_ch_ext[..., reach_x - 2 : wet_ch_ext.shape[2] - reach_x + 2, reach_y - 2 : wet_ch_ext.shape[3] - reach_y + 2, :]
        summed = running
        for substep in range(2):
            fields = ocean_substep_channels(fields, wet, 0.0)
            summed = summed + channel_mean(fields[0:2, :, :, 2 : 2 + size_x, 2 : 2 + size_y])
        keep = fields[..., 1:-1, 1:-1, :]
        return jnp.zeros(shape_late, jnp.float32), keep.reshape(fine_shape), summed / NSUB

    def tracer_b():
        tracer = ext2
        for substep in range(2):
            tracer = tracer_substep(
                tracer,
                trim(wet_coarse_ext, substep + 1, reach_y - mid_y + substep + 1),
                trim(flux_ext, substep + 1, reach_y - mid_y + substep + 1),
                onehot,
                eco_rate,
            )
        absorbed = absorption(trim(tracer, 0, late_y), wet_coarse, above_table)
        outgoing = jnp.broadcast_to(absorbed[None], (2, size_x, size_y, depth))
        return tracer, jnp.zeros(fine_shape, jnp.float32), outgoing

    block_late, ocean_late, outgoing = lax.cond(is_ocean, ocean_b, tracer_b)
    ext3 = halo_x_tracer(block_late, 1)
    arrived = lax.ppermute(outgoing, "half", [(0, 1), (1, 0)])

    def ocean_c():
        light = jnp.pad(arrived[0], ((1, 1), (1, 1), (0, 0)))
        heating = HEATING * jnp.broadcast_to(light, (2, 2) + light.shape)
        wet = wet_ch_ext[..., reach_x - 1 : wet_ch_ext.shape[2] - reach_x + 1, reach_y - 1 : wet_ch_ext.shape[3] - reach_y + 1, :]
        fields = ocean_substep_channels(as_fields(ocean_late), wet, heating)
        return fields[..., 1 : 1 + size_x, 1 : 1 + size_y, :].reshape(channels, size_x, size_y, depth)

    def tracer_c():
        return tracer_substep(trim(ext3, 0, late_y - 1), wet_coarse, arrived, onehot, eco_rate)

    return lax.cond(is_ocean, ocean_c, tracer_c)[None]


def solution(mesh):
    placed = (
        P("half", None, "gx", "gy", None),
        P(None, "gx", "gy"),
        P(None, "gx", "gy", None),
        P(),
        P(),
    )
    return jax.shard_map(
        body,
        mesh=mesh,
        in_specs=placed,
        out_specs=P("half", None, "gx", "gy", None),
        check_vma=False,
    )
```

```python
import jax
import jax.numpy as jnp
from jax import lax
from jax.sharding import PartitionSpec as P

NSUB = 4


DT = 0.1
NU = 1.0
CORIOLIS = 0.5
DRAG = 0.1
MORTALITY = 0.1
HEATING = 2.0
SURFACE = 8.0


def shifts(axis):
    peers = lax.axis_size(axis)
    up = [(i, i + 1) for i in range(peers - 1)]
    down = [(j, i) for i, j in up]
    return up, down


def halo_x(block, cells):
    up, down = shifts("gx")
    before = lax.ppermute(block[:, block.shape[1] - cells :], "gx", up)
    after = lax.ppermute(block[:, :cells], "gx", down)
    return jnp.concatenate([before, block, after], axis=1)


def halo_x_tracer(block, cells):
    peers = lax.axis_size("gx")
    up = [(peers + i, peers + i + 1) for i in range(peers - 1)]
    down = [(j, i) for i, j in up]
    before = lax.ppermute(block[:, block.shape[1] - cells :], ("half", "gx"), up)
    after = lax.ppermute(block[:, :cells], ("half", "gx"), down)
    return jnp.concatenate([before, block, after], axis=1)


def halo_cross(block, rows):
    nx, ny = lax.axis_size("gx"), lax.axis_size("gy")
    size_y = block.shape[2]
    up, down = shifts("gx")
    before = lax.ppermute(block, "gx", up)
    after = lax.ppermute(block, "gx", down)
    up, down = shifts("gy")
    last_rows = block[:, :, size_y - rows :]
    first_rows = block[:, :, :rows]
    below = lax.ppermute(last_rows, "gy", up)
    above = lax.ppermute(first_rows, "gy", down)

    def diagonal(part, dx, dy):
        pairs = [
            (i * ny + j, (i + dx) * ny + j + dy)
            for i in range(nx)
            for j in range(ny)
            if 0 <= i + dx < nx and 0 <= j + dy < ny
        ]
        return lax.ppermute(part, ("gx", "gy"), pairs)

    below_before = diagonal(last_rows, 1, 1)
    below_after = diagonal(last_rows, -1, 1)
    above_before = diagonal(first_rows, 1, -1)
    above_after = diagonal(first_rows, -1, -1)
    middle = jnp.concatenate([before, block, after], axis=1)
    low = jnp.concatenate([below_before, below, below_after], axis=1)
    high = jnp.concatenate([above_before, above, above_after], axis=1)
    return jnp.concatenate([low, middle, high], axis=2)


def halo_y(block, rows):
    up, down = shifts("gy")
    below = lax.ppermute(block[:, :, block.shape[2] - rows :], "gy", up)
    above = lax.ppermute(block[:, :, :rows], "gy", down)
    return jnp.concatenate([below, block, above], axis=2)


def to_fine(coarse):
    fields = coarse.shape[0] // 4
    size_x, size_y, depth = (coarse.shape[1], coarse.shape[2], coarse.shape[3])
    split = coarse.reshape(fields, 2, 2, size_x, size_y, depth).transpose(0, 3, 1, 4, 2, 5)
    return split.reshape(fields, 2 * size_x, 2 * size_y, depth)


def to_coarse(fine_cells):
    fields, fine_x, fine_y, depth = fine_cells.shape
    split = fine_cells.reshape(fields, fine_x // 2, 2, fine_y // 2, 2, depth).transpose(
        0, 2, 4, 1, 3, 5
    )
    return split.reshape(fields * 4, fine_x // 2, fine_y // 2, depth)


def fine_levels(levels):
    size_x, size_y = (levels.shape[1], levels.shape[2])
    return (
        levels.reshape(2, 2, size_x, size_y).transpose(2, 0, 3, 1).reshape(2 * size_x, 2 * size_y)
    )


def wet_of(levels, depth):
    shape = levels.shape + (depth,)
    return (lax.broadcasted_iota(jnp.int32, shape, len(shape) - 1) < levels[..., None]).astype(
        jnp.float32
    )


def wet_of_float(levels, depth):
    shape = levels.shape + (depth,)
    return (
        lax.broadcasted_iota(jnp.int32, shape, len(shape) - 1).astype(jnp.float32)
        < levels[..., None]
    ).astype(jnp.float32)


def trim(values, cut, cut_y=None):
    cut_y = cut if cut_y is None else cut_y
    return values[..., cut : values.shape[-3] - cut, cut_y : values.shape[-2] - cut_y, :]


def ocean_substep(fields, wet_mask, heating):
    centre = fields[:, 1:-1, 1:-1]
    to_east = fields[:, 2:, 1:-1]
    to_west = fields[:, :-2, 1:-1]
    to_north = fields[:, 1:-1, 2:]
    to_south = fields[:, 1:-1, :-2]
    speed_east = centre[0]
    speed_north = centre[1]
    advect = speed_east * (to_east - to_west) * 0.5 + speed_north * (to_north - to_south) * 0.5
    spread = to_east + to_west + to_north + to_south - 4.0 * centre
    zeroes = jnp.zeros_like(speed_east)
    forcing = jnp.stack(
        [
            CORIOLIS * speed_north - DRAG * speed_east,
            -CORIOLIS * speed_east - DRAG * speed_north,
            zeroes + heating,
            zeroes,
            zeroes + 1.0,
        ]
    )
    return wet_mask * (centre + DT * (NU * spread - advect + forcing))


def ocean_substep_channels(fields, wet_mask, heating):
    pad = ((0, 0), (0, 0), (0, 0), (1, 1), (1, 1), (0, 0))
    wide = jnp.pad(fields, pad)
    to_east = jnp.concatenate([fields[:, 1:2], wide[:, 0:1, :, 2:, 1:-1]], axis=1)
    to_west = jnp.concatenate([wide[:, 1:2, :, :-2, 1:-1], fields[:, 0:1]], axis=1)
    to_north = jnp.concatenate([fields[:, :, 1:2], wide[:, :, 0:1, 1:-1, 2:]], axis=2)
    to_south = jnp.concatenate([wide[:, :, 1:2, 1:-1, :-2], fields[:, :, 0:1]], axis=2)
    centre = fields
    speed_east = centre[0]
    speed_north = centre[1]
    advect = speed_east * (to_east - to_west) * 0.5 + speed_north * (to_north - to_south) * 0.5
    spread = to_east + to_west + to_north + to_south - 4.0 * centre
    zeroes = jnp.zeros_like(speed_east)
    forcing = jnp.stack(
        [
            CORIOLIS * speed_north - DRAG * speed_east,
            -CORIOLIS * speed_east - DRAG * speed_north,
            zeroes + heating,
            zeroes,
            zeroes + 1.0,
        ]
    )
    return wet_mask * (centre + DT * (NU * spread - advect + forcing))


def channel_mean(fields):
    coarse = fields.reshape((fields.shape[0], 4) + fields.shape[3:])
    return coarse.sum(axis=1) * 0.25


def tracer_substep(fields, wet_mask, volume_flux, onehot, eco_rate):
    species = eco_rate.shape[0]
    centre = fields[:, 1:-1, 1:-1]
    to_east = fields[:, 2:, 1:-1]
    to_west = fields[:, :-2, 1:-1]
    to_north = fields[:, 1:-1, 2:]
    to_south = fields[:, 1:-1, :-2]
    advect = (
        volume_flux[0] * (to_east - to_west) * 0.5 + volume_flux[1] * (to_north - to_south) * 0.5
    )
    spread = to_east + to_west + to_north + to_south - 4.0 * centre
    living = centre[:species]
    prey_values = jnp.einsum("ts,sxyk->txyk", onehot, living, precision=lax.Precision.HIGHEST)
    growth = eco_rate[:, None, None, None] * living * jnp.tanh(prey_values) - MORTALITY * living
    reaction = jnp.concatenate([growth, jnp.zeros_like(centre[species:])], axis=0)
    return wet_mask * (centre + DT * (NU * spread - advect + reaction))


def coarse_mean(fine_cells):
    coarse = to_coarse(fine_cells)
    return (
        coarse.reshape(
            fine_cells.shape[0], 4, coarse.shape[1], coarse.shape[2], coarse.shape[3]
        ).sum(axis=1)
        * 0.25
    )


def absorption(tracer, wet_mask, above_table):
    attenuation = wet_mask * (0.03 + 0.05 * jax.nn.softplus(tracer[0]))
    overhead = jnp.einsum("xyk,kl->xyl", attenuation, above_table, precision=lax.Precision.HIGHEST)
    return SURFACE * jnp.exp(-overhead) * (1.0 - jnp.exp(-attenuation))


def body(state, levels, old_flux, eco_prey, eco_rate):
    depth = state.shape[-1]
    size_x, size_y = (state.shape[2], state.shape[3])
    species = eco_rate.shape[0]
    channels = state.shape[1]
    is_ocean = lax.axis_index("half") == 0
    level_lanes = jnp.pad(
        levels.astype(jnp.float32).transpose(1, 2, 0), ((0, 0), (0, 0), (0, depth - 4))
    )[None]
    packed = jnp.concatenate([state[0], old_flux, level_lanes], axis=0)
    reach_x, reach_y = size_x, NSUB + 1
    ext1 = halo_cross(packed, reach_y)
    onehot = (eco_prey[:, None] == lax.broadcasted_iota(jnp.int32, (species, species), 1)).astype(
        jnp.float32
    )
    above_table = (
        lax.broadcasted_iota(jnp.int32, (depth, depth), 0)
        < lax.broadcasted_iota(jnp.int32, (depth, depth), 1)
    ).astype(jnp.float32)
    wet_coarse = wet_of(jnp.max(levels, axis=0), depth)
    raw_ext = ext1[:channels]
    flux_ext = ext1[channels : channels + 2]
    levels_ext = ext1[channels + 2, :, :, 0:4].transpose(2, 0, 1)
    wet_coarse_ext = wet_of_float(jnp.max(levels_ext, axis=0), depth)
    zeros_flux = jnp.zeros((2, size_x, size_y, depth), jnp.float32)
    mid_y, late_y = reach_y - 2, reach_y - 4
    shape_mid = (channels, size_x, size_y + 2 * mid_y, depth)
    shape_late = (channels, size_x, size_y + 2 * late_y, depth)

    wet_ch_ext = wet_of_float(levels_ext, depth).reshape((2, 2) + levels_ext.shape[1:] + (depth,))

    def as_fields(block):
        return block.reshape((channels // 4, 2, 2) + block.shape[1:])

    def ocean_a():
        fields = as_fields(raw_ext)[..., 1:-1, 1:-1, :]
        wet = wet_ch_ext[..., 1:-1, 1:-1, :]
        fields = fields * wet[None]
        running = zeros_flux
        for substep in range(2):
            fields = ocean_substep_channels(fields, wet, 0.0)
            running = running + channel_mean(
                fields[0:2, :, :, 1 : 1 + size_x, reach_y - 1 : reach_y - 1 + size_y]
            )
        keep = fields[..., 1 : 1 + size_x, reach_y - 1 - mid_y : reach_y - 1 + size_y + mid_y, :]
        return keep.reshape(shape_mid), running

    def tracer_a():
        tracer = raw_ext * wet_coarse_ext[None]
        for substep in range(2):
            tracer = tracer_substep(
                tracer,
                trim(wet_coarse_ext, substep + 1),
                trim(flux_ext, substep + 1),
                onehot,
                eco_rate,
            )
        return tracer, zeros_flux

    block_mid, running = lax.cond(is_ocean, ocean_a, tracer_a)
    ext2 = halo_x(block_mid, reach_x)
    fine_shape = (channels // 4, 2 * size_x + 2, 2 * size_y + 2, depth)

    fine_shape = (channels, size_x + 2, size_y + 2, depth)

    def ocean_b():
        cut_y = mid_y - 2
        fields = as_fields(ext2)[..., cut_y : ext2.shape[2] - cut_y, :]
        wet = wet_ch_ext[..., reach_x - 2 : wet_ch_ext.shape[2] - reach_x + 2, reach_y - 2 : wet_ch_ext.shape[3] - reach_y + 2, :]
        summed = running
        for substep in range(2):
            fields = ocean_substep_channels(fields, wet, 0.0)
            summed = summed + channel_mean(fields[0:2, :, :, 2 : 2 + size_x, 2 : 2 + size_y])
        keep = fields[..., 1:-1, 1:-1, :]
        return jnp.zeros(shape_late, jnp.float32), keep.reshape(fine_shape), summed / NSUB

    def tracer_b():
        tracer = ext2
        for substep in range(2):
            tracer = tracer_substep(
                tracer,
                trim(wet_coarse_ext, substep + 1, reach_y - mid_y + substep + 1),
                trim(flux_ext, substep + 1, reach_y - mid_y + substep + 1),
                onehot,
                eco_rate,
            )
        absorbed = absorption(trim(tracer, 0, late_y), wet_coarse, above_table)
        outgoing = jnp.broadcast_to(absorbed[None], (2, size_x, size_y, depth))
        return tracer, jnp.zeros(fine_shape, jnp.float32), outgoing

    block_late, ocean_late, outgoing = lax.cond(is_ocean, ocean_b, tracer_b)
    ext3 = halo_x_tracer(block_late, 1)
    arrived = lax.ppermute(outgoing, "half", [(0, 1), (1, 0)])

    def ocean_c():
        light = jnp.pad(arrived[0], ((1, 1), (1, 1), (0, 0)))
        heating = HEATING * jnp.broadcast_to(light, (2, 2) + light.shape)
        wet = wet_ch_ext[..., reach_x - 1 : wet_ch_ext.shape[2] - reach_x + 1, reach_y - 1 : wet_ch_ext.shape[3] - reach_y + 1, :]
        fields = ocean_substep_channels(as_fields(ocean_late), wet, heating)
        return fields[..., 1 : 1 + size_x, 1 : 1 + size_y, :].reshape(channels, size_x, size_y, depth)

    def tracer_c():
        return tracer_substep(trim(ext3, 0, late_y - 1), wet_coarse, arrived, onehot, eco_rate)

    return lax.cond(is_ocean, ocean_c, tracer_c)[None]


def solution(mesh):
    placed = (
        P("half", None, "gx", "gy", None),
        P(None, "gx", "gy"),
        P(None, "gx", "gy", None),
        P(),
        P(),
    )
    return jax.shard_map(
        body,
        mesh=mesh,
        in_specs=placed,
        out_specs=P("half", None, "gx", "gy", None),
        check_vma=False,
    )
```

```python
import jax
import jax.numpy as jnp
from jax import lax
from jax.sharding import PartitionSpec as P

NSUB = 4


DT = 0.1
NU = 1.0
CORIOLIS = 0.5
DRAG = 0.1
MORTALITY = 0.1
HEATING = 2.0
SURFACE = 8.0


def shifts(axis):
    peers = lax.axis_size(axis)
    up = [(i, i + 1) for i in range(peers - 1)]
    down = [(j, i) for i, j in up]
    return up, down


def halo_x(block, cells):
    up, down = shifts("gx")
    before = lax.ppermute(block[:, block.shape[1] - cells :], "gx", up)
    after = lax.ppermute(block[:, :cells], "gx", down)
    return jnp.concatenate([before, block, after], axis=1)


def halo_x_tracer(block, cells):
    peers = lax.axis_size("gx")
    up = [(peers + i, peers + i + 1) for i in range(peers - 1)]
    down = [(j, i) for i, j in up]
    before = lax.ppermute(block[:, block.shape[1] - cells :], ("half", "gx"), up)
    after = lax.ppermute(block[:, :cells], ("half", "gx"), down)
    return jnp.concatenate([before, block, after], axis=1)


def halo_y(block, rows):
    up, down = shifts("gy")
    below = lax.ppermute(block[:, :, block.shape[2] - rows :], "gy", up)
    above = lax.ppermute(block[:, :, :rows], "gy", down)
    return jnp.concatenate([below, block, above], axis=2)


def to_fine(coarse):
    fields = coarse.shape[0] // 4
    size_x, size_y, depth = (coarse.shape[1], coarse.shape[2], coarse.shape[3])
    split = coarse.reshape(fields, 2, 2, size_x, size_y, depth).transpose(0, 3, 1, 4, 2, 5)
    return split.reshape(fields, 2 * size_x, 2 * size_y, depth)


def to_coarse(fine_cells):
    fields, fine_x, fine_y, depth = fine_cells.shape
    split = fine_cells.reshape(fields, fine_x // 2, 2, fine_y // 2, 2, depth).transpose(
        0, 2, 4, 1, 3, 5
    )
    return split.reshape(fields * 4, fine_x // 2, fine_y // 2, depth)


def fine_levels(levels):
    size_x, size_y = (levels.shape[1], levels.shape[2])
    return (
        levels.reshape(2, 2, size_x, size_y).transpose(2, 0, 3, 1).reshape(2 * size_x, 2 * size_y)
    )


def wet_of(levels, depth):
    shape = levels.shape + (depth,)
    return (lax.broadcasted_iota(jnp.int32, shape, len(shape) - 1) < levels[..., None]).astype(
        jnp.float32
    )


def wet_of_float(levels, depth):
    shape = levels.shape + (depth,)
    return (
        lax.broadcasted_iota(jnp.int32, shape, len(shape) - 1).astype(jnp.float32)
        < levels[..., None]
    ).astype(jnp.float32)


def trim(values, cut, cut_y=None):
    cut_y = cut if cut_y is None else cut_y
    return values[..., cut : values.shape[-3] - cut, cut_y : values.shape[-2] - cut_y, :]


def ocean_substep(fields, wet_mask, heating):
    centre = fields[:, 1:-1, 1:-1]
    to_east = fields[:, 2:, 1:-1]
    to_west = fields[:, :-2, 1:-1]
    to_north = fields[:, 1:-1, 2:]
    to_south = fields[:, 1:-1, :-2]
    speed_east = centre[0]
    speed_north = centre[1]
    advect = speed_east * (to_east - to_west) * 0.5 + speed_north * (to_north - to_south) * 0.5
    spread = to_east + to_west + to_north + to_south - 4.0 * centre
    zeroes = jnp.zeros_like(speed_east)
    forcing = jnp.stack(
        [
            CORIOLIS * speed_north - DRAG * speed_east,
            -CORIOLIS * speed_east - DRAG * speed_north,
            zeroes + heating,
            zeroes,
            zeroes + 1.0,
        ]
    )
    return wet_mask * (centre + DT * (NU * spread - advect + forcing))


def ocean_substep_channels(fields, wet_mask, heating):
    pad = ((0, 0), (0, 0), (0, 0), (1, 1), (1, 1), (0, 0))
    wide = jnp.pad(fields, pad)
    to_east = jnp.concatenate([fields[:, 1:2], wide[:, 0:1, :, 2:, 1:-1]], axis=1)
    to_west = jnp.concatenate([wide[:, 1:2, :, :-2, 1:-1], fields[:, 0:1]], axis=1)
    to_north = jnp.concatenate([fields[:, :, 1:2], wide[:, :, 0:1, 1:-1, 2:]], axis=2)
    to_south = jnp.concatenate([wide[:, :, 1:2, 1:-1, :-2], fields[:, :, 0:1]], axis=2)
    centre = fields
    speed_east = centre[0]
    speed_north = centre[1]
    advect = speed_east * (to_east - to_west) * 0.5 + speed_north * (to_north - to_south) * 0.5
    spread = to_east + to_west + to_north + to_south - 4.0 * centre
    zeroes = jnp.zeros_like(speed_east)
    forcing = jnp.stack(
        [
            CORIOLIS * speed_north - DRAG * speed_east,
            -CORIOLIS * speed_east - DRAG * speed_north,
            zeroes + heating,
            zeroes,
            zeroes + 1.0,
        ]
    )
    return wet_mask * (centre + DT * (NU * spread - advect + forcing))


def channel_mean(fields):
    coarse = fields.reshape((fields.shape[0], 4) + fields.shape[3:])
    return coarse.sum(axis=1) * 0.25


def tracer_substep(fields, wet_mask, volume_flux, onehot, eco_rate):
    species = eco_rate.shape[0]
    centre = fields[:, 1:-1, 1:-1]
    to_east = fields[:, 2:, 1:-1]
    to_west = fields[:, :-2, 1:-1]
    to_north = fields[:, 1:-1, 2:]
    to_south = fields[:, 1:-1, :-2]
    advect = (
        volume_flux[0] * (to_east - to_west) * 0.5 + volume_flux[1] * (to_north - to_south) * 0.5
    )
    spread = to_east + to_west + to_north + to_south - 4.0 * centre
    living = centre[:species]
    prey_values = jnp.einsum("ts,sxyk->txyk", onehot, living, precision=lax.Precision.HIGH)
    growth = eco_rate[:, None, None, None] * living * jnp.tanh(prey_values) - MORTALITY * living
    reaction = jnp.concatenate([growth, jnp.zeros_like(centre[species:])], axis=0)
    return wet_mask * (centre + DT * (NU * spread - advect + reaction))


def coarse_mean(fine_cells):
    coarse = to_coarse(fine_cells)
    return (
        coarse.reshape(
            fine_cells.shape[0], 4, coarse.shape[1], coarse.shape[2], coarse.shape[3]
        ).sum(axis=1)
        * 0.25
    )


def absorption(tracer, wet_mask, above_table):
    attenuation = wet_mask * (0.03 + 0.05 * jax.nn.softplus(tracer[0]))
    overhead = jnp.einsum("xyk,kl->xyl", attenuation, above_table, precision=lax.Precision.HIGHEST)
    return SURFACE * jnp.exp(-overhead) * (1.0 - jnp.exp(-attenuation))


def body(state, levels, old_flux, eco_prey, eco_rate):
    depth = state.shape[-1]
    size_x, size_y = (state.shape[2], state.shape[3])
    species = eco_rate.shape[0]
    channels = state.shape[1]
    is_ocean = lax.axis_index("half") == 0
    level_lanes = jnp.pad(
        levels.astype(jnp.float32).transpose(1, 2, 0), ((0, 0), (0, 0), (0, depth - 4))
    )[None]
    packed = jnp.concatenate([state[0], old_flux, level_lanes], axis=0)
    reach_x, reach_y = size_x, NSUB + 1
    ext1 = halo_y(halo_x(packed, reach_x), reach_y)
    onehot = (eco_prey[:, None] == lax.broadcasted_iota(jnp.int32, (species, species), 1)).astype(
        jnp.float32
    )
    above_table = (
        lax.broadcasted_iota(jnp.int32, (depth, depth), 0)
        < lax.broadcasted_iota(jnp.int32, (depth, depth), 1)
    ).astype(jnp.float32)
    wet_coarse = wet_of(jnp.max(levels, axis=0), depth)
    raw_ext = ext1[:channels]
    flux_ext = ext1[channels : channels + 2]
    levels_ext = ext1[channels + 2, :, :, 0:4].transpose(2, 0, 1)
    wet_coarse_ext = wet_of_float(jnp.max(levels_ext, axis=0), depth)
    zeros_flux = jnp.zeros((2, size_x, size_y, depth), jnp.float32)
    mid_y, late_y = reach_y - 2, reach_y - 4
    shape_mid = (channels, size_x, size_y + 2 * mid_y, depth)
    shape_late = (channels, size_x, size_y + 2 * late_y, depth)

    wet_ch_ext = wet_of_float(levels_ext, depth).reshape((2, 2) + levels_ext.shape[1:] + (depth,))

    def as_fields(block):
        return block.reshape((channels // 4, 2, 2) + block.shape[1:])

    def ocean_a():
        fields = as_fields(raw_ext)[..., 1:-1, 1:-1, :]
        wet = wet_ch_ext[..., 1:-1, 1:-1, :]
        fields = fields * wet[None]
        running = zeros_flux
        for substep in range(2):
            fields = ocean_substep_channels(fields, wet, 0.0)
            running = running + channel_mean(
                fields[0:2, :, :, 1 : 1 + size_x, reach_y - 1 : reach_y - 1 + size_y]
            )
        keep = fields[..., 1 : 1 + size_x, reach_y - 1 - mid_y : reach_y - 1 + size_y + mid_y, :]
        return keep.reshape(shape_mid), running

    def tracer_a():
        tracer = raw_ext * wet_coarse_ext[None]
        for substep in range(2):
            tracer = tracer_substep(
                tracer,
                trim(wet_coarse_ext, substep + 1),
                trim(flux_ext, substep + 1),
                onehot,
                eco_rate,
            )
        return tracer, zeros_flux

    block_mid, running = lax.cond(is_ocean, ocean_a, tracer_a)
    ext2 = halo_x(block_mid, reach_x)
    fine_shape = (channels // 4, 2 * size_x + 2, 2 * size_y + 2, depth)

    fine_shape = (channels, size_x + 2, size_y + 2, depth)

    def ocean_b():
        cut_y = mid_y - 2
        fields = as_fields(ext2)[..., cut_y : ext2.shape[2] - cut_y, :]
        wet = wet_ch_ext[..., reach_x - 2 : wet_ch_ext.shape[2] - reach_x + 2, reach_y - 2 : wet_ch_ext.shape[3] - reach_y + 2, :]
        summed = running
        for substep in range(2):
            fields = ocean_substep_channels(fields, wet, 0.0)
            summed = summed + channel_mean(fields[0:2, :, :, 2 : 2 + size_x, 2 : 2 + size_y])
        keep = fields[..., 1:-1, 1:-1, :]
        return jnp.zeros(shape_late, jnp.float32), keep.reshape(fine_shape), summed / NSUB

    def tracer_b():
        tracer = ext2
        for substep in range(2):
            tracer = tracer_substep(
                tracer,
                trim(wet_coarse_ext, substep + 1, reach_y - mid_y + substep + 1),
                trim(flux_ext, substep + 1, reach_y - mid_y + substep + 1),
                onehot,
                eco_rate,
            )
        absorbed = absorption(trim(tracer, 0, late_y), wet_coarse, above_table)
        outgoing = jnp.broadcast_to(absorbed[None], (2, size_x, size_y, depth))
        return tracer, jnp.zeros(fine_shape, jnp.float32), outgoing

    block_late, ocean_late, outgoing = lax.cond(is_ocean, ocean_b, tracer_b)
    ext3 = halo_x_tracer(block_late, 1)
    arrived = lax.ppermute(outgoing, "half", [(0, 1), (1, 0)])

    def ocean_c():
        light = jnp.pad(arrived[0], ((1, 1), (1, 1), (0, 0)))
        heating = HEATING * jnp.broadcast_to(light, (2, 2) + light.shape)
        wet = wet_ch_ext[..., reach_x - 1 : wet_ch_ext.shape[2] - reach_x + 1, reach_y - 1 : wet_ch_ext.shape[3] - reach_y + 1, :]
        fields = ocean_substep_channels(as_fields(ocean_late), wet, heating)
        return fields[..., 1 : 1 + size_x, 1 : 1 + size_y, :].reshape(channels, size_x, size_y, depth)

    def tracer_c():
        return tracer_substep(trim(ext3, 0, late_y - 1), wet_coarse, arrived, onehot, eco_rate)

    return lax.cond(is_ocean, ocean_c, tracer_c)[None]


def solution(mesh):
    placed = (
        P("half", None, "gx", "gy", None),
        P(None, "gx", "gy"),
        P(None, "gx", "gy", None),
        P(),
        P(),
    )
    return jax.shard_map(
        body,
        mesh=mesh,
        in_specs=placed,
        out_specs=P("half", None, "gx", "gy", None),
        check_vma=False,
    )
```

```python
import jax
import jax.numpy as jnp
from jax import lax
from jax.sharding import PartitionSpec as P

NSUB = 4


DT = 0.1
NU = 1.0
CORIOLIS = 0.5
DRAG = 0.1
MORTALITY = 0.1
HEATING = 2.0
SURFACE = 8.0


def shifts(axis):
    peers = lax.axis_size(axis)
    up = [(i, i + 1) for i in range(peers - 1)]
    down = [(j, i) for i, j in up]
    return up, down


def halo_x(block, cells):
    up, down = shifts("gx")
    before = lax.ppermute(block[:, block.shape[1] - cells :], "gx", up)
    after = lax.ppermute(block[:, :cells], "gx", down)
    return jnp.concatenate([before, block, after], axis=1)


def halo_x_tracer(block, cells):
    peers = lax.axis_size("gx")
    up = [(peers + i, peers + i + 1) for i in range(peers - 1)]
    down = [(j, i) for i, j in up]
    before = lax.ppermute(block[:, block.shape[1] - cells :], ("half", "gx"), up)
    after = lax.ppermute(block[:, :cells], ("half", "gx"), down)
    return jnp.concatenate([before, block, after], axis=1)


def halo_y(block, rows):
    up, down = shifts("gy")
    below = lax.ppermute(block[:, :, block.shape[2] - rows :], "gy", up)
    above = lax.ppermute(block[:, :, :rows], "gy", down)
    return jnp.concatenate([below, block, above], axis=2)


def to_fine(coarse):
    fields = coarse.shape[0] // 4
    size_x, size_y, depth = (coarse.shape[1], coarse.shape[2], coarse.shape[3])
    split = coarse.reshape(fields, 2, 2, size_x, size_y, depth).transpose(0, 3, 1, 4, 2, 5)
    return split.reshape(fields, 2 * size_x, 2 * size_y, depth)


def to_coarse(fine_cells):
    fields, fine_x, fine_y, depth = fine_cells.shape
    split = fine_cells.reshape(fields, fine_x // 2, 2, fine_y // 2, 2, depth).transpose(
        0, 2, 4, 1, 3, 5
    )
    return split.reshape(fields * 4, fine_x // 2, fine_y // 2, depth)


def fine_levels(levels):
    size_x, size_y = (levels.shape[1], levels.shape[2])
    return (
        levels.reshape(2, 2, size_x, size_y).transpose(2, 0, 3, 1).reshape(2 * size_x, 2 * size_y)
    )


def wet_of(levels, depth):
    shape = levels.shape + (depth,)
    return (lax.broadcasted_iota(jnp.int32, shape, len(shape) - 1) < levels[..., None]).astype(
        jnp.float32
    )


def wet_of_float(levels, depth):
    shape = levels.shape + (depth,)
    return (
        lax.broadcasted_iota(jnp.int32, shape, len(shape) - 1).astype(jnp.float32)
        < levels[..., None]
    ).astype(jnp.float32)


def trim(values, cut, cut_y=None):
    cut_y = cut if cut_y is None else cut_y
    return values[..., cut : values.shape[-3] - cut, cut_y : values.shape[-2] - cut_y, :]


def ocean_substep(fields, wet_mask, heating):
    centre = fields[:, 1:-1, 1:-1]
    to_east = fields[:, 2:, 1:-1]
    to_west = fields[:, :-2, 1:-1]
    to_north = fields[:, 1:-1, 2:]
    to_south = fields[:, 1:-1, :-2]
    speed_east = centre[0]
    speed_north = centre[1]
    advect = speed_east * (to_east - to_west) * 0.5 + speed_north * (to_north - to_south) * 0.5
    spread = to_east + to_west + to_north + to_south - 4.0 * centre
    zeroes = jnp.zeros_like(speed_east)
    forcing = jnp.stack(
        [
            CORIOLIS * speed_north - DRAG * speed_east,
            -CORIOLIS * speed_east - DRAG * speed_north,
            zeroes + heating,
            zeroes,
            zeroes + 1.0,
        ]
    )
    return wet_mask * (centre + DT * (NU * spread - advect + forcing))


def ocean_substep_channels(fields, wet_mask, heating):
    pad = ((0, 0), (0, 0), (0, 0), (1, 1), (1, 1), (0, 0))
    wide = jnp.pad(fields, pad)
    to_east = jnp.concatenate([fields[:, 1:2], wide[:, 0:1, :, 2:, 1:-1]], axis=1)
    to_west = jnp.concatenate([wide[:, 1:2, :, :-2, 1:-1], fields[:, 0:1]], axis=1)
    to_north = jnp.concatenate([fields[:, :, 1:2], wide[:, :, 0:1, 1:-1, 2:]], axis=2)
    to_south = jnp.concatenate([wide[:, :, 1:2, 1:-1, :-2], fields[:, :, 0:1]], axis=2)
    centre = fields
    speed_east = centre[0]
    speed_north = centre[1]
    advect = speed_east * (to_east - to_west) * 0.5 + speed_north * (to_north - to_south) * 0.5
    spread = to_east + to_west + to_north + to_south - 4.0 * centre
    zeroes = jnp.zeros_like(speed_east)
    forcing = jnp.stack(
        [
            CORIOLIS * speed_north - DRAG * speed_east,
            -CORIOLIS * speed_east - DRAG * speed_north,
            zeroes + heating,
            zeroes,
            zeroes + 1.0,
        ]
    )
    return wet_mask * (centre + DT * (NU * spread - advect + forcing))


def channel_mean(fields):
    coarse = fields.reshape((fields.shape[0], 4) + fields.shape[3:])
    return coarse.sum(axis=1) * 0.25


def tracer_substep(fields, wet_mask, volume_flux, onehot, eco_rate):
    species = eco_rate.shape[0]
    centre = fields[:, 1:-1, 1:-1]
    to_east = fields[:, 2:, 1:-1]
    to_west = fields[:, :-2, 1:-1]
    to_north = fields[:, 1:-1, 2:]
    to_south = fields[:, 1:-1, :-2]
    advect = (
        volume_flux[0] * (to_east - to_west) * 0.5 + volume_flux[1] * (to_north - to_south) * 0.5
    )
    spread = to_east + to_west + to_north + to_south - 4.0 * centre
    living = centre[:species]
    prey_values = jnp.einsum("ts,sxyk->txyk", onehot, living, precision=lax.Precision.HIGH)
    growth = eco_rate[:, None, None, None] * living * jnp.tanh(prey_values) - MORTALITY * living
    reaction = jnp.concatenate([growth, jnp.zeros_like(centre[species:])], axis=0)
    return wet_mask * (centre + DT * (NU * spread - advect + reaction))


def coarse_mean(fine_cells):
    coarse = to_coarse(fine_cells)
    return (
        coarse.reshape(
            fine_cells.shape[0], 4, coarse.shape[1], coarse.shape[2], coarse.shape[3]
        ).sum(axis=1)
        * 0.25
    )


def absorption(tracer, wet_mask, above_table):
    attenuation = wet_mask * (0.03 + 0.05 * jax.nn.softplus(tracer[0]))
    overhead = jnp.einsum("xyk,kl->xyl", attenuation, above_table, precision=lax.Precision.HIGH)
    return SURFACE * jnp.exp(-overhead) * (1.0 - jnp.exp(-attenuation))


def body(state, levels, old_flux, eco_prey, eco_rate):
    depth = state.shape[-1]
    size_x, size_y = (state.shape[2], state.shape[3])
    species = eco_rate.shape[0]
    channels = state.shape[1]
    is_ocean = lax.axis_index("half") == 0
    level_lanes = jnp.pad(
        levels.astype(jnp.float32).transpose(1, 2, 0), ((0, 0), (0, 0), (0, depth - 4))
    )[None]
    packed = jnp.concatenate([state[0], old_flux, level_lanes], axis=0)
    reach_x, reach_y = size_x, NSUB + 1
    ext1 = halo_y(halo_x(packed, reach_x), reach_y)
    onehot = (eco_prey[:, None] == lax.broadcasted_iota(jnp.int32, (species, species), 1)).astype(
        jnp.float32
    )
    above_table = (
        lax.broadcasted_iota(jnp.int32, (depth, depth), 0)
        < lax.broadcasted_iota(jnp.int32, (depth, depth), 1)
    ).astype(jnp.float32)
    wet_coarse = wet_of(jnp.max(levels, axis=0), depth)
    raw_ext = ext1[:channels]
    flux_ext = ext1[channels : channels + 2]
    levels_ext = ext1[channels + 2, :, :, 0:4].transpose(2, 0, 1)
    wet_coarse_ext = wet_of_float(jnp.max(levels_ext, axis=0), depth)
    zeros_flux = jnp.zeros((2, size_x, size_y, depth), jnp.float32)
    mid_y, late_y = reach_y - 2, reach_y - 4
    shape_mid = (channels, size_x, size_y + 2 * mid_y, depth)
    shape_late = (channels, size_x, size_y + 2 * late_y, depth)

    wet_ch_ext = wet_of_float(levels_ext, depth).reshape((2, 2) + levels_ext.shape[1:] + (depth,))

    def as_fields(block):
        return block.reshape((channels // 4, 2, 2) + block.shape[1:])

    def ocean_a():
        fields = as_fields(raw_ext)[..., 1:-1, 1:-1, :]
        wet = wet_ch_ext[..., 1:-1, 1:-1, :]
        fields = fields * wet[None]
        running = zeros_flux
        for substep in range(2):
            fields = ocean_substep_channels(fields, wet, 0.0)
            running = running + channel_mean(
                fields[0:2, :, :, 1 : 1 + size_x, reach_y - 1 : reach_y - 1 + size_y]
            )
        keep = fields[..., 1 : 1 + size_x, reach_y - 1 - mid_y : reach_y - 1 + size_y + mid_y, :]
        return keep.reshape(shape_mid), running

    def tracer_a():
        tracer = raw_ext * wet_coarse_ext[None]
        for substep in range(2):
            tracer = tracer_substep(
                tracer,
                trim(wet_coarse_ext, substep + 1),
                trim(flux_ext, substep + 1),
                onehot,
                eco_rate,
            )
        return tracer, zeros_flux

    block_mid, running = lax.cond(is_ocean, ocean_a, tracer_a)
    ext2 = halo_x(block_mid, reach_x)
    fine_shape = (channels // 4, 2 * size_x + 2, 2 * size_y + 2, depth)

    fine_shape = (channels, size_x + 2, size_y + 2, depth)

    def ocean_b():
        cut_y = mid_y - 2
        fields = as_fields(ext2)[..., cut_y : ext2.shape[2] - cut_y, :]
        wet = wet_ch_ext[..., reach_x - 2 : wet_ch_ext.shape[2] - reach_x + 2, reach_y - 2 : wet_ch_ext.shape[3] - reach_y + 2, :]
        summed = running
        for substep in range(2):
            fields = ocean_substep_channels(fields, wet, 0.0)
            summed = summed + channel_mean(fields[0:2, :, :, 2 : 2 + size_x, 2 : 2 + size_y])
        keep = fields[..., 1:-1, 1:-1, :]
        return jnp.zeros(shape_late, jnp.float32), keep.reshape(fine_shape), summed / NSUB

    def tracer_b():
        tracer = ext2
        for substep in range(2):
            tracer = tracer_substep(
                tracer,
                trim(wet_coarse_ext, substep + 1, reach_y - mid_y + substep + 1),
                trim(flux_ext, substep + 1, reach_y - mid_y + substep + 1),
                onehot,
                eco_rate,
            )
        absorbed = absorption(trim(tracer, 0, late_y), wet_coarse, above_table)
        outgoing = jnp.broadcast_to(absorbed[None], (2, size_x, size_y, depth))
        return tracer, jnp.zeros(fine_shape, jnp.float32), outgoing

    block_late, ocean_late, outgoing = lax.cond(is_ocean, ocean_b, tracer_b)
    ext3 = halo_x_tracer(block_late, 1)
    arrived = lax.ppermute(outgoing, "half", [(0, 1), (1, 0)])

    def ocean_c():
        light = jnp.pad(arrived[0], ((1, 1), (1, 1), (0, 0)))
        heating = HEATING * jnp.broadcast_to(light, (2, 2) + light.shape)
        wet = wet_ch_ext[..., reach_x - 1 : wet_ch_ext.shape[2] - reach_x + 1, reach_y - 1 : wet_ch_ext.shape[3] - reach_y + 1, :]
        fields = ocean_substep_channels(as_fields(ocean_late), wet, heating)
        return fields[..., 1 : 1 + size_x, 1 : 1 + size_y, :].reshape(channels, size_x, size_y, depth)

    def tracer_c():
        return tracer_substep(trim(ext3, 0, late_y - 1), wet_coarse, arrived, onehot, eco_rate)

    return lax.cond(is_ocean, ocean_c, tracer_c)[None]


def solution(mesh):
    placed = (
        P("half", None, "gx", "gy", None),
        P(None, "gx", "gy"),
        P(None, "gx", "gy", None),
        P(),
        P(),
    )
    return jax.shard_map(
        body,
        mesh=mesh,
        in_specs=placed,
        out_specs=P("half", None, "gx", "gy", None),
        check_vma=False,
    )
```

```python
import jax
import jax.numpy as jnp
from jax import lax
from jax.sharding import PartitionSpec as P

NSUB = 4


DT = 0.1
NU = 1.0
CORIOLIS = 0.5
DRAG = 0.1
MORTALITY = 0.1
HEATING = 2.0
SURFACE = 8.0


def shifts(axis):
    peers = lax.axis_size(axis)
    up = [(i, i + 1) for i in range(peers - 1)]
    down = [(j, i) for i, j in up]
    return up, down


def halo_x(block, cells):
    up, down = shifts("gx")
    before = lax.ppermute(block[:, block.shape[1] - cells :], "gx", up)
    after = lax.ppermute(block[:, :cells], "gx", down)
    return jnp.concatenate([before, block, after], axis=1)


def halo_x_tracer(block, cells):
    peers = lax.axis_size("gx")
    up = [(peers + i, peers + i + 1) for i in range(peers - 1)]
    down = [(j, i) for i, j in up]
    before = lax.ppermute(block[:, block.shape[1] - cells :], ("half", "gx"), up)
    after = lax.ppermute(block[:, :cells], ("half", "gx"), down)
    return jnp.concatenate([before, block, after], axis=1)


def halo_y(block, rows):
    up, down = shifts("gy")
    below = lax.ppermute(block[:, :, block.shape[2] - rows :], "gy", up)
    above = lax.ppermute(block[:, :, :rows], "gy", down)
    return jnp.concatenate([below, block, above], axis=2)


def to_fine(coarse):
    fields = coarse.shape[0] // 4
    size_x, size_y, depth = (coarse.shape[1], coarse.shape[2], coarse.shape[3])
    split = coarse.reshape(fields, 2, 2, size_x, size_y, depth).transpose(0, 3, 1, 4, 2, 5)
    return split.reshape(fields, 2 * size_x, 2 * size_y, depth)


def to_coarse(fine_cells):
    fields, fine_x, fine_y, depth = fine_cells.shape
    split = fine_cells.reshape(fields, fine_x // 2, 2, fine_y // 2, 2, depth).transpose(
        0, 2, 4, 1, 3, 5
    )
    return split.reshape(fields * 4, fine_x // 2, fine_y // 2, depth)


def fine_levels(levels):
    size_x, size_y = (levels.shape[1], levels.shape[2])
    return (
        levels.reshape(2, 2, size_x, size_y).transpose(2, 0, 3, 1).reshape(2 * size_x, 2 * size_y)
    )


def wet_of(levels, depth):
    shape = levels.shape + (depth,)
    return (lax.broadcasted_iota(jnp.int32, shape, len(shape) - 1) < levels[..., None]).astype(
        jnp.float32
    )


def wet_of_float(levels, depth):
    shape = levels.shape + (depth,)
    return (
        lax.broadcasted_iota(jnp.int32, shape, len(shape) - 1).astype(jnp.float32)
        < levels[..., None]
    ).astype(jnp.float32)


def trim(values, cut, cut_y=None):
    cut_y = cut if cut_y is None else cut_y
    return values[..., cut : values.shape[-3] - cut, cut_y : values.shape[-2] - cut_y, :]


def ocean_substep(fields, wet_mask, heating):
    centre = fields[:, 1:-1, 1:-1]
    to_east = fields[:, 2:, 1:-1]
    to_west = fields[:, :-2, 1:-1]
    to_north = fields[:, 1:-1, 2:]
    to_south = fields[:, 1:-1, :-2]
    speed_east = centre[0]
    speed_north = centre[1]
    advect = speed_east * (to_east - to_west) * 0.5 + speed_north * (to_north - to_south) * 0.5
    spread = to_east + to_west + to_north + to_south - 4.0 * centre
    zeroes = jnp.zeros_like(speed_east)
    forcing = jnp.stack(
        [
            CORIOLIS * speed_north - DRAG * speed_east,
            -CORIOLIS * speed_east - DRAG * speed_north,
            zeroes + heating,
            zeroes,
            zeroes + 1.0,
        ]
    )
    return wet_mask * (centre + DT * (NU * spread - advect + forcing))


def ocean_substep_channels(fields, wet_mask, heating):
    pad = ((0, 0), (0, 0), (0, 0), (1, 1), (1, 1), (0, 0))
    wide = jnp.pad(fields, pad)
    to_east = jnp.concatenate([fields[:, 1:2], wide[:, 0:1, :, 2:, 1:-1]], axis=1)
    to_west = jnp.concatenate([wide[:, 1:2, :, :-2, 1:-1], fields[:, 0:1]], axis=1)
    to_north = jnp.concatenate([fields[:, :, 1:2], wide[:, :, 0:1, 1:-1, 2:]], axis=2)
    to_south = jnp.concatenate([wide[:, :, 1:2, 1:-1, :-2], fields[:, :, 0:1]], axis=2)
    centre = fields
    speed_east = centre[0]
    speed_north = centre[1]
    advect = speed_east * (to_east - to_west) * 0.5 + speed_north * (to_north - to_south) * 0.5
    spread = to_east + to_west + to_north + to_south - 4.0 * centre
    zeroes = jnp.zeros_like(speed_east)
    forcing = jnp.stack(
        [
            CORIOLIS * speed_north - DRAG * speed_east,
            -CORIOLIS * speed_east - DRAG * speed_north,
            zeroes + heating,
            zeroes,
            zeroes + 1.0,
        ]
    )
    return wet_mask * (centre + DT * (NU * spread - advect + forcing))


def channel_mean(fields):
    coarse = fields.reshape((fields.shape[0], 4) + fields.shape[3:])
    return coarse.sum(axis=1) * 0.25


def tracer_substep(fields, wet_mask, volume_flux, onehot, eco_rate):
    species = eco_rate.shape[0]
    centre = fields[:, 1:-1, 1:-1]
    to_east = fields[:, 2:, 1:-1]
    to_west = fields[:, :-2, 1:-1]
    to_north = fields[:, 1:-1, 2:]
    to_south = fields[:, 1:-1, :-2]
    advect = (
        volume_flux[0] * (to_east - to_west) * 0.5 + volume_flux[1] * (to_north - to_south) * 0.5
    )
    spread = to_east + to_west + to_north + to_south - 4.0 * centre
    living = centre[:species]
    prey_values = jnp.einsum("ts,sxyk->txyk", onehot, living, precision=lax.Precision.HIGH)
    growth = eco_rate[:, None, None, None] * living * jnp.tanh(prey_values) - MORTALITY * living
    reaction = jnp.concatenate([growth, jnp.zeros_like(centre[species:])], axis=0)
    return wet_mask * (centre + DT * (NU * spread - advect + reaction))


def coarse_mean(fine_cells):
    coarse = to_coarse(fine_cells)
    return (
        coarse.reshape(
            fine_cells.shape[0], 4, coarse.shape[1], coarse.shape[2], coarse.shape[3]
        ).sum(axis=1)
        * 0.25
    )


def absorption(tracer, wet_mask, above_table):
    attenuation = wet_mask * (0.03 + 0.05 * jax.nn.softplus(tracer[0]))
    overhead = jnp.einsum("xyk,kl->xyl", attenuation, above_table, precision=lax.Precision.HIGHEST)
    return SURFACE * jnp.exp(-overhead) * (1.0 - jnp.exp(-attenuation))


def body(state, levels, old_flux, eco_prey, eco_rate):
    depth = state.shape[-1]
    size_x, size_y = (state.shape[2], state.shape[3])
    species = eco_rate.shape[0]
    channels = state.shape[1]
    is_ocean = lax.axis_index("half") == 0
    lane_group = depth // 4
    level_lanes = jnp.concatenate(
        [
            jnp.broadcast_to(levels[c].astype(jnp.float32)[:, :, None], (size_x, size_y, lane_group))
            for c in range(4)
        ],
        axis=-1,
    )[None]
    packed = jnp.concatenate([state[0], old_flux, level_lanes], axis=0)
    reach_x, reach_y = size_x, NSUB + 1
    ext1 = halo_y(halo_x(packed, reach_x), reach_y)
    onehot = (eco_prey[:, None] == lax.broadcasted_iota(jnp.int32, (species, species), 1)).astype(
        jnp.float32
    )
    above_table = (
        lax.broadcasted_iota(jnp.int32, (depth, depth), 0)
        < lax.broadcasted_iota(jnp.int32, (depth, depth), 1)
    ).astype(jnp.float32)
    wet_coarse = wet_of(jnp.max(levels, axis=0), depth)
    raw_ext = ext1[:channels]
    flux_ext = ext1[channels : channels + 2]
    levels_ext = ext1[channels + 2, :, :, ::lane_group].transpose(2, 0, 1)
    wet_coarse_ext = wet_of_float(jnp.max(levels_ext, axis=0), depth)
    zeros_flux = jnp.zeros((2, size_x, size_y, depth), jnp.float32)
    mid_y, late_y = reach_y - 2, reach_y - 4
    shape_mid = (channels, size_x, size_y + 2 * mid_y, depth)
    shape_late = (channels, size_x, size_y + 2 * late_y, depth)

    wet_ch_ext = wet_of_float(levels_ext, depth).reshape((2, 2) + levels_ext.shape[1:] + (depth,))

    def as_fields(block):
        return block.reshape((channels // 4, 2, 2) + block.shape[1:])

    def ocean_a():
        fields = as_fields(raw_ext)[..., 1:-1, 1:-1, :]
        wet = wet_ch_ext[..., 1:-1, 1:-1, :]
        fields = fields * wet[None]
        running = zeros_flux
        for substep in range(2):
            fields = ocean_substep_channels(fields, wet, 0.0)
            running = running + channel_mean(
                fields[0:2, :, :, 1 : 1 + size_x, reach_y - 1 : reach_y - 1 + size_y]
            )
        keep = fields[..., 1 : 1 + size_x, reach_y - 1 - mid_y : reach_y - 1 + size_y + mid_y, :]
        return keep.reshape(shape_mid), running

    def tracer_a():
        tracer = raw_ext * wet_coarse_ext[None]
        for substep in range(2):
            tracer = tracer_substep(
                tracer,
                trim(wet_coarse_ext, substep + 1),
                trim(flux_ext, substep + 1),
                onehot,
                eco_rate,
            )
        return tracer, zeros_flux

    block_mid, running = lax.cond(is_ocean, ocean_a, tracer_a)
    ext2 = halo_x(block_mid, reach_x)
    fine_shape = (channels // 4, 2 * size_x + 2, 2 * size_y + 2, depth)

    fine_shape = (channels, size_x + 2, size_y + 2, depth)

    def ocean_b():
        cut_y = mid_y - 2
        fields = as_fields(ext2)[..., cut_y : ext2.shape[2] - cut_y, :]
        wet = wet_ch_ext[..., reach_x - 2 : wet_ch_ext.shape[2] - reach_x + 2, reach_y - 2 : wet_ch_ext.shape[3] - reach_y + 2, :]
        summed = running
        for substep in range(2):
            fields = ocean_substep_channels(fields, wet, 0.0)
            summed = summed + channel_mean(fields[0:2, :, :, 2 : 2 + size_x, 2 : 2 + size_y])
        keep = fields[..., 1:-1, 1:-1, :]
        return jnp.zeros(shape_late, jnp.float32), keep.reshape(fine_shape), summed / NSUB

    def tracer_b():
        tracer = ext2
        for substep in range(2):
            tracer = tracer_substep(
                tracer,
                trim(wet_coarse_ext, substep + 1, reach_y - mid_y + substep + 1),
                trim(flux_ext, substep + 1, reach_y - mid_y + substep + 1),
                onehot,
                eco_rate,
            )
        absorbed = absorption(trim(tracer, 0, late_y), wet_coarse, above_table)
        outgoing = jnp.broadcast_to(absorbed[None], (2, size_x, size_y, depth))
        return tracer, jnp.zeros(fine_shape, jnp.float32), outgoing

    block_late, ocean_late, outgoing = lax.cond(is_ocean, ocean_b, tracer_b)
    ext3 = halo_x_tracer(block_late, 1)
    arrived = lax.ppermute(outgoing, "half", [(0, 1), (1, 0)])

    def ocean_c():
        light = jnp.pad(arrived[0], ((1, 1), (1, 1), (0, 0)))
        heating = HEATING * jnp.broadcast_to(light, (2, 2) + light.shape)
        wet = wet_ch_ext[..., reach_x - 1 : wet_ch_ext.shape[2] - reach_x + 1, reach_y - 1 : wet_ch_ext.shape[3] - reach_y + 1, :]
        fields = ocean_substep_channels(as_fields(ocean_late), wet, heating)
        return fields[..., 1 : 1 + size_x, 1 : 1 + size_y, :].reshape(channels, size_x, size_y, depth)

    def tracer_c():
        return tracer_substep(trim(ext3, 0, late_y - 1), wet_coarse, arrived, onehot, eco_rate)

    return lax.cond(is_ocean, ocean_c, tracer_c)[None]


def solution(mesh):
    placed = (
        P("half", None, "gx", "gy", None),
        P(None, "gx", "gy"),
        P(None, "gx", "gy", None),
        P(),
        P(),
    )
    return jax.shard_map(
        body,
        mesh=mesh,
        in_specs=placed,
        out_specs=P("half", None, "gx", "gy", None),
        check_vma=False,
    )
```

```python
import jax
import jax.numpy as jnp
from jax import lax
from jax.sharding import PartitionSpec as P

NSUB = 4


DT = 0.1
NU = 1.0
CORIOLIS = 0.5
DRAG = 0.1
MORTALITY = 0.1
HEATING = 2.0
SURFACE = 8.0


def shifts(axis):
    peers = lax.axis_size(axis)
    up = [(i, i + 1) for i in range(peers - 1)]
    down = [(j, i) for i, j in up]
    return up, down


def halo_x(block, cells):
    up, down = shifts("gx")
    before = lax.ppermute(block[:, block.shape[1] - cells :], "gx", up)
    after = lax.ppermute(block[:, :cells], "gx", down)
    return jnp.concatenate([before, block, after], axis=1)


def halo_x_tracer(block, cells):
    peers = lax.axis_size("gx")
    up = [(peers + i, peers + i + 1) for i in range(peers - 1)]
    down = [(j, i) for i, j in up]
    before = lax.ppermute(block[:, block.shape[1] - cells :], ("half", "gx"), up)
    after = lax.ppermute(block[:, :cells], ("half", "gx"), down)
    return jnp.concatenate([before, block, after], axis=1)


def halo_y(block, rows):
    up, down = shifts("gy")
    below = lax.ppermute(block[:, :, block.shape[2] - rows :], "gy", up)
    above = lax.ppermute(block[:, :, :rows], "gy", down)
    return jnp.concatenate([below, block, above], axis=2)


def to_fine(coarse):
    fields = coarse.shape[0] // 4
    size_x, size_y, depth = (coarse.shape[1], coarse.shape[2], coarse.shape[3])
    split = coarse.reshape(fields, 2, 2, size_x, size_y, depth).transpose(0, 3, 1, 4, 2, 5)
    return split.reshape(fields, 2 * size_x, 2 * size_y, depth)


def to_coarse(fine_cells):
    fields, fine_x, fine_y, depth = fine_cells.shape
    split = fine_cells.reshape(fields, fine_x // 2, 2, fine_y // 2, 2, depth).transpose(
        0, 2, 4, 1, 3, 5
    )
    return split.reshape(fields * 4, fine_x // 2, fine_y // 2, depth)


def fine_levels(levels):
    size_x, size_y = (levels.shape[1], levels.shape[2])
    return (
        levels.reshape(2, 2, size_x, size_y).transpose(2, 0, 3, 1).reshape(2 * size_x, 2 * size_y)
    )


def wet_of(levels, depth):
    shape = levels.shape + (depth,)
    return (lax.broadcasted_iota(jnp.int32, shape, len(shape) - 1) < levels[..., None]).astype(
        jnp.float32
    )


def wet_of_float(levels, depth):
    shape = levels.shape + (depth,)
    return (
        lax.broadcasted_iota(jnp.int32, shape, len(shape) - 1).astype(jnp.float32)
        < levels[..., None]
    ).astype(jnp.float32)


def trim(values, cut, cut_y=None):
    cut_y = cut if cut_y is None else cut_y
    return values[..., cut : values.shape[-3] - cut, cut_y : values.shape[-2] - cut_y, :]


def ocean_substep(fields, wet_mask, heating):
    centre = fields[:, 1:-1, 1:-1]
    to_east = fields[:, 2:, 1:-1]
    to_west = fields[:, :-2, 1:-1]
    to_north = fields[:, 1:-1, 2:]
    to_south = fields[:, 1:-1, :-2]
    speed_east = centre[0]
    speed_north = centre[1]
    advect = speed_east * (to_east - to_west) * 0.5 + speed_north * (to_north - to_south) * 0.5
    spread = to_east + to_west + to_north + to_south - 4.0 * centre
    zeroes = jnp.zeros_like(speed_east)
    forcing = jnp.stack(
        [
            CORIOLIS * speed_north - DRAG * speed_east,
            -CORIOLIS * speed_east - DRAG * speed_north,
            zeroes + heating,
            zeroes,
            zeroes + 1.0,
        ]
    )
    return wet_mask * (centre + DT * (NU * spread - advect + forcing))


def ocean_substep_channels(fields, wet_mask, heating):
    pad = ((0, 0), (0, 0), (0, 0), (1, 1), (1, 1), (0, 0))
    wide = jnp.pad(fields, pad)
    to_east = jnp.concatenate([fields[:, 1:2], wide[:, 0:1, :, 2:, 1:-1]], axis=1)
    to_west = jnp.concatenate([wide[:, 1:2, :, :-2, 1:-1], fields[:, 0:1]], axis=1)
    to_north = jnp.concatenate([fields[:, :, 1:2], wide[:, :, 0:1, 1:-1, 2:]], axis=2)
    to_south = jnp.concatenate([wide[:, :, 1:2, 1:-1, :-2], fields[:, :, 0:1]], axis=2)
    centre = fields
    speed_east = centre[0]
    speed_north = centre[1]
    advect = speed_east * (to_east - to_west) * 0.5 + speed_north * (to_north - to_south) * 0.5
    spread = to_east + to_west + to_north + to_south - 4.0 * centre
    zeroes = jnp.zeros_like(speed_east)
    forcing = jnp.stack(
        [
            CORIOLIS * speed_north - DRAG * speed_east,
            -CORIOLIS * speed_east - DRAG * speed_north,
            zeroes + heating,
            zeroes,
            zeroes + 1.0,
        ]
    )
    return wet_mask * (centre + DT * (NU * spread - advect + forcing))


def channel_mean(fields):
    coarse = fields.reshape((fields.shape[0], 4) + fields.shape[3:])
    return coarse.sum(axis=1) * 0.25


def tracer_substep(fields, wet_mask, volume_flux, onehot, eco_rate):
    species = eco_rate.shape[0]
    centre = fields[:, 1:-1, 1:-1]
    to_east = fields[:, 2:, 1:-1]
    to_west = fields[:, :-2, 1:-1]
    to_north = fields[:, 1:-1, 2:]
    to_south = fields[:, 1:-1, :-2]
    advect = (
        volume_flux[0] * (to_east - to_west) * 0.5 + volume_flux[1] * (to_north - to_south) * 0.5
    )
    spread = to_east + to_west + to_north + to_south - 4.0 * centre
    living = centre[:species]
    prey_values = jnp.einsum("ts,sxyk->txyk", onehot, living, precision=lax.Precision.HIGH)
    growth = eco_rate[:, None, None, None] * living * jnp.tanh(prey_values) - MORTALITY * living
    reaction = jnp.concatenate([growth, jnp.zeros_like(centre[species:])], axis=0)
    return wet_mask * (centre + DT * (NU * spread - advect + reaction))


def coarse_mean(fine_cells):
    coarse = to_coarse(fine_cells)
    return (
        coarse.reshape(
            fine_cells.shape[0], 4, coarse.shape[1], coarse.shape[2], coarse.shape[3]
        ).sum(axis=1)
        * 0.25
    )


def absorption(tracer, wet_mask, above_table):
    attenuation = wet_mask * (0.03 + 0.05 * jax.nn.softplus(tracer[0]))
    overhead = jnp.einsum("xyk,kl->xyl", attenuation, above_table, precision=lax.Precision.HIGHEST)
    return SURFACE * jnp.exp(-overhead) * (1.0 - jnp.exp(-attenuation))


def body(state, levels, old_flux, eco_prey, eco_rate):
    depth = state.shape[-1]
    size_x, size_y = (state.shape[2], state.shape[3])
    species = eco_rate.shape[0]
    channels = state.shape[1]
    is_ocean = lax.axis_index("half") == 0
    level_lanes = jnp.pad(
        levels.astype(jnp.float32).transpose(1, 2, 0), ((0, 0), (0, 0), (0, depth - 4))
    )[None]
    own_wet = jnp.where(
        is_ocean,
        wet_of(levels, depth)[None].repeat(channels // 4, axis=0).reshape(channels, size_x, size_y, depth),
        jnp.broadcast_to(wet_of(jnp.max(levels, axis=0), depth), (channels, size_x, size_y, depth)),
    )
    packed = jnp.concatenate([state[0] * own_wet, old_flux, level_lanes], axis=0)
    reach_x, reach_y = size_x, NSUB + 1
    ext1 = halo_y(halo_x(packed, reach_x), reach_y)
    onehot = (eco_prey[:, None] == lax.broadcasted_iota(jnp.int32, (species, species), 1)).astype(
        jnp.float32
    )
    above_table = (
        lax.broadcasted_iota(jnp.int32, (depth, depth), 0)
        < lax.broadcasted_iota(jnp.int32, (depth, depth), 1)
    ).astype(jnp.float32)
    wet_coarse = wet_of(jnp.max(levels, axis=0), depth)
    raw_ext = ext1[:channels]
    flux_ext = ext1[channels : channels + 2]
    levels_ext = ext1[channels + 2, :, :, 0:4].transpose(2, 0, 1)
    wet_coarse_ext = wet_of_float(jnp.max(levels_ext, axis=0), depth)
    zeros_flux = jnp.zeros((2, size_x, size_y, depth), jnp.float32)
    mid_y, late_y = reach_y - 2, reach_y - 4
    shape_mid = (channels, size_x, size_y + 2 * mid_y, depth)
    shape_late = (channels, size_x, size_y + 2 * late_y, depth)

    wet_ch_ext = wet_of_float(levels_ext, depth).reshape((2, 2) + levels_ext.shape[1:] + (depth,))

    def as_fields(block):
        return block.reshape((channels // 4, 2, 2) + block.shape[1:])

    def ocean_a():
        fields = as_fields(raw_ext)[..., 1:-1, 1:-1, :]
        wet = wet_ch_ext[..., 1:-1, 1:-1, :]
        running = zeros_flux
        for substep in range(2):
            fields = ocean_substep_channels(fields, wet, 0.0)
            running = running + channel_mean(
                fields[0:2, :, :, 1 : 1 + size_x, reach_y - 1 : reach_y - 1 + size_y]
            )
        keep = fields[..., 1 : 1 + size_x, reach_y - 1 - mid_y : reach_y - 1 + size_y + mid_y, :]
        return keep.reshape(shape_mid), running

    def tracer_a():
        tracer = raw_ext
        for substep in range(2):
            tracer = tracer_substep(
                tracer,
                trim(wet_coarse_ext, substep + 1),
                trim(flux_ext, substep + 1),
                onehot,
                eco_rate,
            )
        return tracer, zeros_flux

    block_mid, running = lax.cond(is_ocean, ocean_a, tracer_a)
    ext2 = halo_x(block_mid, reach_x)
    fine_shape = (channels // 4, 2 * size_x + 2, 2 * size_y + 2, depth)

    fine_shape = (channels, size_x + 2, size_y + 2, depth)

    def ocean_b():
        cut_y = mid_y - 2
        fields = as_fields(ext2)[..., cut_y : ext2.shape[2] - cut_y, :]
        wet = wet_ch_ext[..., reach_x - 2 : wet_ch_ext.shape[2] - reach_x + 2, reach_y - 2 : wet_ch_ext.shape[3] - reach_y + 2, :]
        summed = running
        for substep in range(2):
            fields = ocean_substep_channels(fields, wet, 0.0)
            summed = summed + channel_mean(fields[0:2, :, :, 2 : 2 + size_x, 2 : 2 + size_y])
        keep = fields[..., 1:-1, 1:-1, :]
        return jnp.zeros(shape_late, jnp.float32), keep.reshape(fine_shape), summed / NSUB

    def tracer_b():
        tracer = ext2
        for substep in range(2):
            tracer = tracer_substep(
                tracer,
                trim(wet_coarse_ext, substep + 1, reach_y - mid_y + substep + 1),
                trim(flux_ext, substep + 1, reach_y - mid_y + substep + 1),
                onehot,
                eco_rate,
            )
        absorbed = absorption(trim(tracer, 0, late_y), wet_coarse, above_table)
        outgoing = jnp.broadcast_to(absorbed[None], (2, size_x, size_y, depth))
        return tracer, jnp.zeros(fine_shape, jnp.float32), outgoing

    block_late, ocean_late, outgoing = lax.cond(is_ocean, ocean_b, tracer_b)
    ext3 = halo_x_tracer(block_late, 1)
    arrived = lax.ppermute(outgoing, "half", [(0, 1), (1, 0)])

    def ocean_c():
        light = jnp.pad(arrived[0], ((1, 1), (1, 1), (0, 0)))
        heating = HEATING * jnp.broadcast_to(light, (2, 2) + light.shape)
        wet = wet_ch_ext[..., reach_x - 1 : wet_ch_ext.shape[2] - reach_x + 1, reach_y - 1 : wet_ch_ext.shape[3] - reach_y + 1, :]
        fields = ocean_substep_channels(as_fields(ocean_late), wet, heating)
        return fields[..., 1 : 1 + size_x, 1 : 1 + size_y, :].reshape(channels, size_x, size_y, depth)

    def tracer_c():
        return tracer_substep(trim(ext3, 0, late_y - 1), wet_coarse, arrived, onehot, eco_rate)

    return lax.cond(is_ocean, ocean_c, tracer_c)[None]


def solution(mesh):
    placed = (
        P("half", None, "gx", "gy", None),
        P(None, "gx", "gy"),
        P(None, "gx", "gy", None),
        P(),
        P(),
    )
    return jax.shard_map(
        body,
        mesh=mesh,
        in_specs=placed,
        out_specs=P("half", None, "gx", "gy", None),
        check_vma=False,
    )
```

```python
import jax
import jax.numpy as jnp
from jax import lax
from jax.sharding import PartitionSpec as P

NSUB = 4


DT = 0.1
NU = 1.0
CORIOLIS = 0.5
DRAG = 0.1
MORTALITY = 0.1
HEATING = 2.0
SURFACE = 8.0


def shifts(axis):
    peers = lax.axis_size(axis)
    up = [(i, i + 1) for i in range(peers - 1)]
    down = [(j, i) for i, j in up]
    return up, down


def halo_x(block, cells):
    up, down = shifts("gx")
    before = lax.ppermute(block[:, block.shape[1] - cells :], "gx", up)
    after = lax.ppermute(block[:, :cells], "gx", down)
    return jnp.concatenate([before, block, after], axis=1)


def halo_x_tracer(block, cells):
    peers = lax.axis_size("gx")
    up = [(peers + i, peers + i + 1) for i in range(peers - 1)]
    down = [(j, i) for i, j in up]
    before = lax.ppermute(block[:, block.shape[1] - cells :], ("half", "gx"), up)
    after = lax.ppermute(block[:, :cells], ("half", "gx"), down)
    return jnp.concatenate([before, block, after], axis=1)


def halo_y(block, rows):
    up, down = shifts("gy")
    below = lax.ppermute(block[:, :, block.shape[2] - rows :], "gy", up)
    above = lax.ppermute(block[:, :, :rows], "gy", down)
    return jnp.concatenate([below, block, above], axis=2)


def to_fine(coarse):
    fields = coarse.shape[0] // 4
    size_x, size_y, depth = (coarse.shape[1], coarse.shape[2], coarse.shape[3])
    split = coarse.reshape(fields, 2, 2, size_x, size_y, depth).transpose(0, 3, 1, 4, 2, 5)
    return split.reshape(fields, 2 * size_x, 2 * size_y, depth)


def to_coarse(fine_cells):
    fields, fine_x, fine_y, depth = fine_cells.shape
    split = fine_cells.reshape(fields, fine_x // 2, 2, fine_y // 2, 2, depth).transpose(
        0, 2, 4, 1, 3, 5
    )
    return split.reshape(fields * 4, fine_x // 2, fine_y // 2, depth)


def fine_levels(levels):
    size_x, size_y = (levels.shape[1], levels.shape[2])
    return (
        levels.reshape(2, 2, size_x, size_y).transpose(2, 0, 3, 1).reshape(2 * size_x, 2 * size_y)
    )


def wet_of(levels, depth):
    shape = levels.shape + (depth,)
    return (lax.broadcasted_iota(jnp.int32, shape, len(shape) - 1) < levels[..., None]).astype(
        jnp.float32
    )


def wet_of_float(levels, depth):
    shape = levels.shape + (depth,)
    return (
        lax.broadcasted_iota(jnp.int32, shape, len(shape) - 1).astype(jnp.float32)
        < levels[..., None]
    ).astype(jnp.float32)


def trim(values, cut, cut_y=None):
    cut_y = cut if cut_y is None else cut_y
    return values[..., cut : values.shape[-3] - cut, cut_y : values.shape[-2] - cut_y, :]


def ocean_substep(fields, wet_mask, heating):
    centre = fields[:, 1:-1, 1:-1]
    to_east = fields[:, 2:, 1:-1]
    to_west = fields[:, :-2, 1:-1]
    to_north = fields[:, 1:-1, 2:]
    to_south = fields[:, 1:-1, :-2]
    speed_east = centre[0]
    speed_north = centre[1]
    advect = speed_east * (to_east - to_west) * 0.5 + speed_north * (to_north - to_south) * 0.5
    spread = to_east + to_west + to_north + to_south - 4.0 * centre
    zeroes = jnp.zeros_like(speed_east)
    forcing = jnp.stack(
        [
            CORIOLIS * speed_north - DRAG * speed_east,
            -CORIOLIS * speed_east - DRAG * speed_north,
            zeroes + heating,
            zeroes,
            zeroes + 1.0,
        ]
    )
    return wet_mask * (centre + DT * (NU * spread - advect + forcing))


def ocean_substep_channels(fields, wet_mask, heating):
    pad = ((0, 0), (0, 0), (0, 0), (1, 1), (1, 1), (0, 0))
    wide = jnp.pad(fields, pad)
    to_east = jnp.concatenate([fields[:, 1:2], wide[:, 0:1, :, 2:, 1:-1]], axis=1)
    to_west = jnp.concatenate([wide[:, 1:2, :, :-2, 1:-1], fields[:, 0:1]], axis=1)
    to_north = jnp.concatenate([fields[:, :, 1:2], wide[:, :, 0:1, 1:-1, 2:]], axis=2)
    to_south = jnp.concatenate([wide[:, :, 1:2, 1:-1, :-2], fields[:, :, 0:1]], axis=2)
    centre = fields
    speed_east = centre[0]
    speed_north = centre[1]
    advect = speed_east * (to_east - to_west) * 0.5 + speed_north * (to_north - to_south) * 0.5
    spread = to_east + to_west + to_north + to_south - 4.0 * centre
    zeroes = jnp.zeros_like(speed_east)
    forcing = jnp.stack(
        [
            CORIOLIS * speed_north - DRAG * speed_east,
            -CORIOLIS * speed_east - DRAG * speed_north,
            zeroes + heating,
            zeroes,
            zeroes + 1.0,
        ]
    )
    return wet_mask * (centre + DT * (NU * spread - advect + forcing))


def channel_mean(fields):
    coarse = fields.reshape((fields.shape[0], 4) + fields.shape[3:])
    return coarse.sum(axis=1) * 0.25


def tracer_substep(fields, wet_mask, volume_flux, onehot, eco_rate):
    species = eco_rate.shape[0]
    centre = fields[:, 1:-1, 1:-1]
    to_east = fields[:, 2:, 1:-1]
    to_west = fields[:, :-2, 1:-1]
    to_north = fields[:, 1:-1, 2:]
    to_south = fields[:, 1:-1, :-2]
    advect = (
        volume_flux[0] * (to_east - to_west) * 0.5 + volume_flux[1] * (to_north - to_south) * 0.5
    )
    spread = to_east + to_west + to_north + to_south - 4.0 * centre
    living = centre[:species]
    prey_values = jnp.einsum("ts,sxyk->txyk", onehot, living, precision=lax.Precision.HIGH)
    growth = eco_rate[:, None, None, None] * living * jnp.tanh(prey_values) - MORTALITY * living
    reaction = jnp.concatenate([growth, jnp.zeros_like(centre[species:])], axis=0)
    return wet_mask * (centre + DT * (NU * spread - advect + reaction))


def coarse_mean(fine_cells):
    coarse = to_coarse(fine_cells)
    return (
        coarse.reshape(
            fine_cells.shape[0], 4, coarse.shape[1], coarse.shape[2], coarse.shape[3]
        ).sum(axis=1)
        * 0.25
    )


def absorption(tracer, wet_mask, above_table):
    attenuation = wet_mask * (0.03 + 0.05 * jax.nn.softplus(tracer[0]))
    overhead = jnp.einsum("xyk,kl->xyl", attenuation, above_table, precision=lax.Precision.HIGHEST)
    return SURFACE * jnp.exp(-overhead) * (1.0 - jnp.exp(-attenuation))


def body(state, levels, old_flux, eco_prey, eco_rate):
    depth = state.shape[-1]
    size_x, size_y = (state.shape[2], state.shape[3])
    species = eco_rate.shape[0]
    channels = state.shape[1]
    is_ocean = lax.axis_index("half") == 0
    level_lanes = jnp.pad(
        levels.astype(jnp.float32).transpose(1, 2, 0), ((0, 0), (0, 0), (0, depth - 4))
    )[None]
    packed = jnp.concatenate([state[0], old_flux, level_lanes], axis=0)
    reach_x, reach_y = size_x, NSUB + 1
    ext1 = halo_y(halo_x(packed, reach_x), reach_y)
    onehot = (eco_prey[:, None] == lax.broadcasted_iota(jnp.int32, (species, species), 1)).astype(
        jnp.float32
    )
    above_table = (
        lax.broadcasted_iota(jnp.int32, (depth, depth), 0)
        < lax.broadcasted_iota(jnp.int32, (depth, depth), 1)
    ).astype(jnp.float32)
    wet_coarse = wet_of(jnp.max(levels, axis=0), depth)
    raw_ext = ext1[:channels]
    flux_ext = ext1[channels : channels + 2]
    levels_ext = ext1[channels + 2, :, :, 0:4].transpose(2, 0, 1)
    wet_coarse_ext = wet_of_float(jnp.max(levels_ext, axis=0), depth)
    zeros_flux = jnp.zeros((2, size_x, size_y, depth), jnp.float32)
    mid_y, late_y = reach_y - 2, reach_y - 4
    shape_mid = (channels, size_x, size_y + 2 * mid_y, depth)
    shape_late = (channels, size_x, size_y + 2 * late_y, depth)

    wet_ch_ext = wet_of_float(levels_ext, depth).reshape((2, 2) + levels_ext.shape[1:] + (depth,))

    def as_fields(block):
        return block.reshape((channels // 4, 2, 2) + block.shape[1:])

    def ocean_a():
        fields = as_fields(raw_ext)[..., 1:-1, 1:-1, :]
        wet = wet_ch_ext[..., 1:-1, 1:-1, :]
        fields = fields * wet[None]
        running = zeros_flux
        for substep in range(2):
            fields = ocean_substep_channels(fields, wet, 0.0)
            running = running + channel_mean(
                fields[0:2, :, :, 1 : 1 + size_x, reach_y - 1 : reach_y - 1 + size_y]
            )
        keep = fields[..., 1 : 1 + size_x, reach_y - 1 - mid_y : reach_y - 1 + size_y + mid_y, :]
        return keep.reshape(shape_mid), running

    def tracer_a():
        tracer = raw_ext * wet_coarse_ext[None]
        for substep in range(2):
            tracer = tracer_substep(
                tracer,
                trim(wet_coarse_ext, substep + 1),
                trim(flux_ext, substep + 1),
                onehot,
                eco_rate,
            )
        return tracer, zeros_flux

    block_mid, running = lax.cond(is_ocean, ocean_a, tracer_a)
    ext2 = halo_x(block_mid, reach_x)
    fine_shape = (channels // 4, 2 * size_x + 2, 2 * size_y + 2, depth)

    fine_shape = (channels, size_x + 2, size_y + 2, depth)

    def ocean_b():
        cut_y = mid_y - 2
        fields = as_fields(ext2)[..., cut_y : ext2.shape[2] - cut_y, :]
        wet = wet_ch_ext[..., reach_x - 2 : wet_ch_ext.shape[2] - reach_x + 2, reach_y - 2 : wet_ch_ext.shape[3] - reach_y + 2, :]
        summed = running
        for substep in range(2):
            fields = ocean_substep_channels(fields, wet, 0.0)
            summed = summed + channel_mean(fields[0:2, :, :, 2 : 2 + size_x, 2 : 2 + size_y])
        keep = fields[..., 1:-1, 1:-1, :]
        return jnp.zeros(shape_late, jnp.float32), keep.reshape(fine_shape), summed / NSUB

    def tracer_b():
        tracer = ext2
        for substep in range(2):
            tracer = tracer_substep(
                tracer,
                trim(wet_coarse_ext, substep + 1, reach_y - mid_y + substep + 1),
                trim(flux_ext, substep + 1, reach_y - mid_y + substep + 1),
                onehot,
                eco_rate,
            )
        chlorophyll = trim(tracer, 0, late_y)[0]
        outgoing = jnp.broadcast_to(chlorophyll[None], (2, size_x, size_y, depth))
        return tracer, jnp.zeros(fine_shape, jnp.float32), outgoing

    block_late, ocean_late, outgoing = lax.cond(is_ocean, ocean_b, tracer_b)
    ext3 = halo_x_tracer(block_late, 1)
    arrived = lax.ppermute(outgoing, "half", [(0, 1), (1, 0)])

    def ocean_c():
        light = jnp.pad(absorption(arrived, wet_coarse, above_table), ((1, 1), (1, 1), (0, 0)))
        heating = HEATING * jnp.broadcast_to(light, (2, 2) + light.shape)
        wet = wet_ch_ext[..., reach_x - 1 : wet_ch_ext.shape[2] - reach_x + 1, reach_y - 1 : wet_ch_ext.shape[3] - reach_y + 1, :]
        fields = ocean_substep_channels(as_fields(ocean_late), wet, heating)
        return fields[..., 1 : 1 + size_x, 1 : 1 + size_y, :].reshape(channels, size_x, size_y, depth)

    def tracer_c():
        return tracer_substep(trim(ext3, 0, late_y - 1), wet_coarse, arrived, onehot, eco_rate)

    return lax.cond(is_ocean, ocean_c, tracer_c)[None]


def solution(mesh):
    placed = (
        P("half", None, "gx", "gy", None),
        P(None, "gx", "gy"),
        P(None, "gx", "gy", None),
        P(),
        P(),
    )
    return jax.shard_map(
        body,
        mesh=mesh,
        in_specs=placed,
        out_specs=P("half", None, "gx", "gy", None),
        check_vma=False,
    )
```
